512 devices in a mesh: gx: 128 (over z_lo, x, y), gy: 2 (over core), gz: 2 (over z_hi).
Axes of the slice: x: 4, y: 8, z: 8 (z_hi: 2, z_lo: 4; z = z_hi * 4 + z_lo), core: 2. Of those that a mesh axis runs over, the one named last changes fastest.
Arguments:
- velocity: bfloat16 [3, 256, 16, 256], P(None, 'gx', 'gy', 'gz'), may hold values from -6 to 6
- eddy_viscosity: float32 [256, 16, 256], P('gx', 'gy', 'gz'), may hold values from 0.02 to 0.3
- cell_owner: int32 [2, 2, 262144, 1], P('gy', 'gz', 'gx'), may hold values from 0 to 127; in each aligned block of 2048 rows (0 to 2047, 2048 to 4095, ..., all dimensions but the last counted through in order) at most 24 rows name the same one
- cell_element: int32 [2, 2, 262144], P('gy', 'gz', 'gx'), may hold values from 0 to 3
- cell_position: int32 [2, 2, 262144], P('gy', 'gz', 'gx'), may hold values from 0 to 4095
- acoustic_state: float32 [4, 128, 2, 8, 512], P(None, 'gx', 'gy', 'gz'), may hold values from -6 to 6
Outputs:
- source_moments: float32 [128, 2, 8, 3, 512], P('gx', 'gy', 'gz')
- next_state: float32 [4, 128, 2, 8, 512], P(None, 'gx', 'gy', 'gz')
The draws below stay inside these ranges and needn't reach their ends.
Inputs may be any that keep to these rules, and one draw needn't show every extreme that they name: `cell_owner`: in the rows of one device (aligned blocks of 2048 rows along the last two dimensions), no owner is named more than 24 times, a bound that some block reaches.
All inputs are finite; a program needn't handle non-finite values.
Results may differ from the reference program's by a relative error of at most 0.0039.
Values may be sent and summed in bfloat16 or wider, within the bound.
No kernel may reach another device: no remote copies, remote signals or barrier semaphores. Data moves between devices by JAX's collectives and lax.ppermute only.
A program may use at most 64 MiB of HBM per device.

```python
import math
import jax
import jax.numpy as jnp
import numpy as np
from jax import lax

CX = 2
CY = 8
CZ = 128
EX = 1
EY = 1
EZ = 4
SUB = 16
NODES = 512
CELLS = 2048
CAP = 24
ELEMS_DEV = 4
NX = 256
NY = 16
NZ = 256
EGX = 128
EGY = 2
EGZ = 8
N_GX = 128
N_GY = 2
N_GZ = 2


def plant(values, rng, least, top_value):
    place = [jax.random.randint(jax.random.fold_in(rng, axis), (), 0, length) for axis, length in enumerate(values.shape)]
    widest = values.shape.index(max(values.shape))
    beside = place[:widest] + [(place[widest] + 1) % values.shape[widest]] + place[widest + 1:]
    return values.at[tuple(place)].set(least).at[tuple(beside)].set(top_value)


def block_scale(key, shape, shards, smallest, high):
    def one(position, parts):
        steps = jax.random.uniform(jax.random.fold_in(jax.random.fold_in(key, 6), position), (parts,), jnp.float32, smallest / len(shards), high / len(shards))
        return jnp.repeat(jnp.exp(steps), shape[position] // parts).reshape((-1,) + (1,) * (len(shape) - position - 1))

    loudness = one(*shards[0])
    for cut in shards[1:]:
        loudness = loudness * one(*cut)
    return loudness


def shared_out(stream_key, own, number, rows, number_of, top, bound, slope):
    sequence = jax.random.permutation(stream_key, number_of)
    packed, common = shares(number_of, rows * top, bound, slope, True), shares(number_of, rows * top, bound, slope, False)
    places = jnp.arange(number_of)

    def named(sizes, offset_by):
        used = int((sizes > 0).sum())
        fixed = max(1, used // 4)
        moved = fixed + (places - fixed + offset_by * (used - fixed)) % max(1, number_of - fixed)
        return jnp.zeros((number_of,), jnp.int32).at[sequence[jnp.where(places < fixed, places, moved)]].set(jnp.asarray(sizes, jnp.int32))

    sizes = jnp.where(number % 4 == 0, named(packed, number // 4), named(common, number - number // 4 - 1))
    mixed = jax.random.permutation(jax.random.fold_in(own, 3), number_of)
    giver, taker = mixed[0:number_of // 2 * 2:2], mixed[1:number_of // 2 * 2:2]
    slack = jnp.minimum(sizes[giver] - 1, bound - sizes[taker]) // 2
    slack = jnp.where((giver == sequence[0]) | (taker == sequence[0]) | (sizes[taker] == 0), 0, jnp.maximum(slack, 0))
    moved = jax.random.randint(jax.random.fold_in(own, 4), (number_of // 2,), 0, 1 << 20) % (slack + 1)
    sizes = sizes.at[giver].add(-moved).at[taker].add(moved)
    members = jnp.searchsorted(jnp.cumsum(sizes), jnp.arange(rows * top), side="right").astype(jnp.int32)
    table = members.reshape(top, rows).T
    table = table[jax.random.permutation(jax.random.fold_in(own, 1), rows)]
    offset_by = jax.random.randint(jax.random.fold_in(own, 2), (rows, 1), 0, top)
    return jnp.take_along_axis(table, (jnp.arange(top)[None, :] + offset_by) % top, axis=1)


def shares(count, total, limit, slope, full):
    weights = [(1 << 20) // math.isqrt(standing ** slope) + 1 for standing in range(1, count + 1)]
    largest = limit if full else min(limit, max(-(-total // count), total * weights[0] // sum(weights)))
    least = 1 if total - largest >= count - 1 else 0
    given, surplus = [largest] + [least] * (count - 1), total - largest - least * (count - 1)
    while surplus > 0:
        movable = [i for i in range(1, count) if given[i] < largest] or [i for i in range(1, count) if given[i] < limit]
        pool, left = sum([weights[i] for i in movable]), surplus
        for i in movable:
            more = min(limit - given[i], max(1, left * weights[i] // pool), surplus)
            given[i] = given[i] + more
            surplus = surplus - more
    return np.array(given)


def centred(rng, dims, deviation, reach, split=(), kind=jnp.bfloat16):
    drawn = jax.random.normal(rng, dims, jnp.float32) * deviation
    if len(split) > 0:
        drawn = block_scale(rng, dims, split, -0.22, 0.18) * drawn
    return jnp.clip(drawn, min=-reach, max=reach).astype(kind)


def setup_inputs(seed: int = 0) -> dict:
    seeds = jax.random.split(jax.random.key(seed), 7)
    velocity = centred(seeds[0], (3, NX, NY, NZ), 1.0, 6.0, ((1, 128), (2, 2), (3, 2)))
    eddy_viscosity = jnp.clip(jnp.exp(math.log(0.3) - 2.7080503 * jax.random.uniform(seeds[1], (NX, NY, NZ), jnp.float32) ** block_scale(seeds[1], (NX, NY, NZ), ((0, 128), (1, 2), (2, 2)), -0.2, 0.2)), 0.02, 0.3)
    cell_owner_keys = jax.random.split(jax.random.fold_in(seeds[2], 1), N_GY * N_GZ * (N_GX * CELLS) // CELLS)
    cell_owner_turns = jax.random.permutation(jax.random.fold_in(seeds[2], 3), N_GY * N_GZ * (N_GX * CELLS) // CELLS)
    cell_owner = jax.vmap(lambda own, number: shared_out(jax.random.fold_in(seeds[2], 2), own, number, CELLS, N_GX, 1, CAP, 1))(cell_owner_keys, cell_owner_turns).reshape((N_GY, N_GZ, N_GX * CELLS, 1))
    cell_element = plant(jax.random.randint(seeds[3], (N_GY, N_GZ, N_GX * CELLS), 0, ELEMS_DEV), jax.random.fold_in(seeds[3], 1), 0, ELEMS_DEV - 1).astype(jnp.int32)
    cell_position = plant(jax.random.randint(seeds[4], (N_GY, N_GZ, N_GX * CELLS), 0, SUB * SUB * SUB), jax.random.fold_in(seeds[4], 1), 0, (SUB * SUB * SUB) - 1).astype(jnp.int32)
    acoustic_state = centred(seeds[5], (4, EGX, EGY, EGZ, NODES), 1.0, 6.0, ((1, 128), (2, 2), (3, 2)), jnp.float32)
    return {"velocity": velocity, "eddy_viscosity": eddy_viscosity, "cell_owner": cell_owner, "cell_element": cell_element, "cell_position": cell_position, "acoustic_state": acoustic_state}


GLL_POINTS = np.array([-1.0, -0.8717401485096066, -0.5917001814331423, -0.2092992179024789, 0.2092992179024789, 0.5917001814331423, 0.8717401485096066, 1.0])
LIFT_FACTOR = 28.0
TIME_STEP = 0.01
COUPLING = 4.0
MOMENT_WEIGHT = 0.0625


def derivative_matrix():
    points = GLL_POINTS
    barycentric = np.ones(8)
    for j in range(8):
        for m in range(8):
            if m != j:
                barycentric[j] = barycentric[j] / (points[j] - points[m])
    matrix = np.zeros((8, 8))
    for i in range(8):
        for j in range(8):
            if i != j:
                matrix[i, j] = barycentric[j] / barycentric[i] / (points[i] - points[j])
        matrix[i, i] = -np.sum(matrix[i])
    return matrix


def kron_tables():
    matrix = derivative_matrix()
    identity = np.eye(8)
    along_x = np.kron(np.kron(matrix, identity), identity).T
    along_y = np.kron(np.kron(identity, matrix), identity).T
    along_z = np.kron(np.kron(identity, identity), matrix).T
    return [jnp.asarray(t, dtype=jnp.float32) for t in (along_x, along_y, along_z)]


def basis_table():
    points = GLL_POINTS
    centres = -1.0 + (2.0 * np.arange(SUB) + 1.0) / SUB
    values = np.ones((SUB, 8))
    for j in range(8):
        for m in range(8):
            if m != j:
                values[:, j] = values[:, j] * (centres - points[m]) / (points[j] - points[m])
    return jnp.asarray(values, dtype=jnp.float32)


def source_from_padded(padded, viscosity):
    centre = padded[:, 1:-1, 1:-1, 1:-1]
    plus_x = padded[:, 2:, 1:-1, 1:-1]
    minus_x = padded[:, :-2, 1:-1, 1:-1]
    plus_y = padded[:, 1:-1, 2:, 1:-1]
    minus_y = padded[:, 1:-1, :-2, 1:-1]
    plus_z = padded[:, 1:-1, 1:-1, 2:]
    minus_z = padded[:, 1:-1, 1:-1, :-2]
    grad_x = 0.5 * (plus_x - minus_x)
    grad_y = 0.5 * (plus_y - minus_y)
    grad_z = 0.5 * (plus_z - minus_z)
    laplace = plus_x + minus_x + plus_y + minus_y + plus_z + minus_z - 6.0 * centre
    curl_x = grad_y[2] - grad_z[1]
    curl_y = grad_z[0] - grad_x[2]
    curl_z = grad_x[1] - grad_y[0]
    lamb_x = curl_y * centre[2] - curl_z * centre[1]
    lamb_y = curl_z * centre[0] - curl_x * centre[2]
    lamb_z = curl_x * centre[1] - curl_y * centre[0]
    lamb = jnp.stack([lamb_x, lamb_y, lamb_z])
    return (viscosity[None] * laplace - lamb).astype(jnp.bfloat16)


def face_correction(inside, outside, normal, component):
    difference = inside - outside
    result = -0.5 * difference
    result = result.at[0].add(0.5 * normal * difference[component])
    result = result.at[component].add(0.5 * normal * difference[0])
    return LIFT_FACTOR * result


def tendency(fields, forcing, tables, exterior):
    highest = lax.Precision.HIGHEST
    pressure = fields[0]
    grad_x = jnp.dot(pressure, tables[0], precision=highest)
    grad_y = jnp.dot(pressure, tables[1], precision=highest)
    grad_z = jnp.dot(pressure, tables[2], precision=highest)
    divergence = jnp.dot(fields[1], tables[0], precision=highest) + jnp.dot(fields[2], tables[1], precision=highest) + jnp.dot(fields[3], tables[2], precision=highest)
    result = jnp.stack([-divergence, COUPLING * forcing[0] - grad_x, COUPLING * forcing[1] - grad_y, COUPLING * forcing[2] - grad_z])
    shape_now = fields.shape
    nodal_view = fields.reshape(shape_now[:4] + (8, 8, 8))
    result = result.reshape(nodal_view.shape)
    for direction in range(3):
        node_axis = 4 + direction
        lower_face = jnp.take(nodal_view, 0, axis=node_axis)
        upper_face = jnp.take(nodal_view, 7, axis=node_axis)
        lower_outer, upper_outer = exterior(lower_face, upper_face, direction)
        leading = (slice(None),) * node_axis
        result = result.at[leading + (0,)].add(face_correction(lower_face, lower_outer, -1.0, direction + 1))
        result = result.at[leading + (7,)].add(face_correction(upper_face, upper_outer, 1.0, direction + 1))
    return result.reshape(shape_now)


def runge_kutta(fields, forcing, exterior):
    tables = kron_tables()
    section_one = fields + TIME_STEP * tendency(fields, forcing, tables, exterior)
    section_two = 0.75 * fields + 0.25 * (section_one + TIME_STEP * tendency(section_one, forcing, tables, exterior))
    return (1.0 / 3.0) * fields + (2.0 / 3.0) * (section_two + TIME_STEP * tendency(section_two, forcing, tables, exterior))


def zero_exterior(lower_face, upper_face, direction):
    elem_axis = direction + 1
    extent = lower_face.shape[elem_axis]
    zero_rim = jnp.zeros_like(lax.slice_in_dim(lower_face, 0, 1, axis=elem_axis))
    lower_outer = jnp.concatenate([zero_rim, lax.slice_in_dim(upper_face, 0, extent - 1, axis=elem_axis)], axis=elem_axis)
    upper_outer = jnp.concatenate([lax.slice_in_dim(lower_face, 1, extent, axis=elem_axis), zero_rim], axis=elem_axis)
    return lower_outer, upper_outer


def position_rows():
    values = basis_table()
    node_rows = (values[:, None, None, :, None, None] * values[None, :, None, None, :, None]) * values[None, None, :, None, None, :]
    return node_rows.reshape(SUB * SUB * SUB, NODES).astype(jnp.bfloat16)


def reference(velocity, eddy_viscosity, cell_owner, cell_element, cell_position, acoustic_state):
    padded = jnp.pad(velocity.astype(jnp.float32), ((0, 0), (1, 1), (1, 1), (1, 1)))
    sources = source_from_padded(padded, eddy_viscosity)
    columns = N_GY * N_GZ
    cell_count = CX * CY * CZ
    subcells = SUB * SUB * SUB
    ordered = sources.astype(jnp.float32).reshape(3, N_GX, CX, N_GY, CY, N_GZ, CZ)
    ordered = jnp.transpose(ordered, (3, 5, 1, 2, 4, 6, 0)).reshape(columns, N_GX * cell_count, 3)
    owners = cell_owner.reshape(columns, N_GX * cell_count)
    elements = cell_element.reshape(columns, N_GX * cell_count)
    positions = cell_position.reshape(columns, N_GX * cell_count)
    weight_rows = position_rows().astype(jnp.float32)

    def column_moments(column_items):
        column_source, column_owner, column_element, column_position = column_items
        segment_ids = (column_owner * ELEMS_DEV + column_element) * subcells + column_position
        totals = jax.ops.segment_sum(column_source, segment_ids, num_segments=N_GX * ELEMS_DEV * subcells)
        totals = totals.reshape(N_GX * ELEMS_DEV, subcells, 3)
        return jnp.einsum('gpc,pn->gcn', totals, weight_rows, precision=lax.Precision.HIGHEST)

    moments = lax.map(column_moments, (ordered, owners, elements, positions))
    moments = moments * MOMENT_WEIGHT
    moments = moments.reshape(N_GY, N_GZ, N_GX, EX, EY, EZ, 3, NODES)
    moments = jnp.transpose(moments, (2, 3, 0, 4, 1, 5, 6, 7)).reshape(EGX, EGY, EGZ, 3, NODES)
    forcing = jnp.moveaxis(moments, 3, 0)
    next_state = runge_kutta(acoustic_state, forcing, zero_exterior)
    return moments, next_state
```

```python
import jax
import jax.numpy as jnp
import numpy as np
from jax import lax
from jax.sharding import PartitionSpec as P

SUB = 16
NODES = 512


GLL_POINTS = np.array(
    [
        -1.0,
        -0.8717401485096066,
        -0.5917001814331423,
        -0.2092992179024789,
        0.2092992179024789,
        0.5917001814331423,
        0.8717401485096066,
        1.0,
    ]
)
LIFT_FACTOR = 28.0
TIME_STEP = 0.01
COUPLING = 4.0
MOMENT_WEIGHT = 0.0625


def derivative_matrix():
    points = GLL_POINTS
    barycentric = np.ones(8)
    for j in range(8):
        for m in range(8):
            if m != j:
                barycentric[j] = barycentric[j] / (points[j] - points[m])
    matrix = np.zeros((8, 8))
    for i in range(8):
        for j in range(8):
            if i != j:
                matrix[i, j] = barycentric[j] / barycentric[i] / (points[i] - points[j])
        matrix[i, i] = -np.sum(matrix[i])
    return matrix


def kron_tables():
    matrix, identity = lax.optimization_barrier(
        (jnp.asarray(derivative_matrix().T, jnp.float32), jnp.eye(8, dtype=jnp.float32))
    )
    d = matrix
    e = identity
    along_x = d[:, None, None, :, None, None] * e[None, :, None, None, :, None]
    along_x = along_x * e[None, None, :, None, None, :]
    along_y = e[:, None, None, :, None, None] * d[None, :, None, None, :, None]
    along_y = along_y * e[None, None, :, None, None, :]
    along_z = e[:, None, None, :, None, None] * e[None, :, None, None, :, None]
    along_z = along_z * d[None, None, :, None, None, :]
    return [t.reshape(NODES, NODES) for t in (along_x, along_y, along_z)]


def basis_table():
    points = GLL_POINTS
    centres = -1.0 + (2.0 * np.arange(SUB) + 1.0) / SUB
    values = np.ones((SUB, 8))
    for j in range(8):
        for m in range(8):
            if m != j:
                values[:, j] = values[:, j] * (centres - points[m]) / (points[j] - points[m])
    return np.asarray(values, dtype=np.float32)


def neighbours(lower, upper, axis):
    count = lax.axis_size(axis)
    if count == 1:
        return jnp.zeros_like(upper), jnp.zeros_like(lower)
    if count == 2:
        index = lax.axis_index(axis)
        sent = jnp.where(index == 0, upper, lower)
        got = lax.ppermute(sent, axis, [(0, 1), (1, 0)])
        zero = jnp.zeros_like(got)
        return jnp.where(index == 1, got, zero), jnp.where(index == 0, got, zero)
    from_below = lax.ppermute(upper, axis, [(i, i + 1) for i in range(count - 1)])
    from_above = lax.ppermute(lower, axis, [(i + 1, i) for i in range(count - 1)])
    return from_below, from_above


def source_cells(velocity, viscosity):
    below_x, above_x = neighbours(velocity[:, :1], velocity[:, -1:], "gx")
    below_y, above_y = neighbours(velocity[:, :, :1], velocity[:, :, -1:], "gy")
    below_z, above_z = neighbours(velocity[..., :1], velocity[..., -1:], "gz")
    centre = velocity.astype(jnp.float32)
    f32 = lambda t: t.astype(jnp.float32)
    plus_x = jnp.concatenate([centre[:, 1:], f32(above_x)], axis=1)
    minus_x = jnp.concatenate([f32(below_x), centre[:, :-1]], axis=1)
    plus_y = jnp.concatenate([centre[:, :, 1:], f32(above_y)], axis=2)
    minus_y = jnp.concatenate([f32(below_y), centre[:, :, :-1]], axis=2)
    plus_z = jnp.concatenate([centre[..., 1:], f32(above_z)], axis=3)
    minus_z = jnp.concatenate([f32(below_z), centre[..., :-1]], axis=3)
    grad_x = 0.5 * (plus_x - minus_x)
    grad_y = 0.5 * (plus_y - minus_y)
    grad_z = 0.5 * (plus_z - minus_z)
    laplace = plus_x + minus_x + plus_y + minus_y + plus_z + minus_z - 6.0 * centre
    curl_x = grad_y[2] - grad_z[1]
    curl_y = grad_z[0] - grad_x[2]
    curl_z = grad_x[1] - grad_y[0]
    lamb_x = curl_y * centre[2] - curl_z * centre[1]
    lamb_y = curl_z * centre[0] - curl_x * centre[2]
    lamb_z = curl_x * centre[1] - curl_y * centre[0]
    lamb = jnp.stack([lamb_x, lamb_y, lamb_z])
    return (viscosity[None] * laplace - lamb).astype(jnp.bfloat16)


def face_correction(inside, outside, normal, component):
    difference = inside - outside
    result = -0.5 * difference
    first = result[0] + 0.5 * normal * difference[component]
    chosen = result[component] + 0.5 * normal * difference[0]
    parts = [result[i] for i in range(4)]
    parts[0] = first
    parts[component] = chosen
    return LIFT_FACTOR * jnp.stack(parts)


def tendency(fields, forcing, grad_table, div_table):
    highest = lax.Precision.HIGHEST
    count = fields.shape[1]
    flat = fields.reshape(4, count, NODES)
    grads = [jnp.dot(flat[0], table, precision=highest) for table in div_table]
    divergence = (
        jnp.dot(flat[1], div_table[0], precision=highest)
        + jnp.dot(flat[2], div_table[1], precision=highest)
        + jnp.dot(flat[3], div_table[2], precision=highest)
    )
    result = jnp.stack(
        [
            -divergence,
            COUPLING * forcing[0] - grads[0],
            COUPLING * forcing[1] - grads[1],
            COUPLING * forcing[2] - grads[2],
        ]
    ).reshape(fields.shape)

    lower_x = fields[:, :, 0]
    upper_x = fields[:, :, 7]
    lower_y = fields[:, :, :, 0]
    upper_y = fields[:, :, :, 7]
    lower_z = fields[..., 0]
    upper_z = fields[..., 7]
    below_x, above_x = neighbours(lower_x, upper_x, "gx")
    below_y, above_y = neighbours(lower_y, upper_y, "gy")
    below_z, above_z = neighbours(lower_z[:, :1], upper_z[:, -1:], "gz")
    outer_lower_z = jnp.concatenate([below_z, upper_z[:, :-1]], axis=1)
    outer_upper_z = jnp.concatenate([lower_z[:, 1:], above_z], axis=1)

    node = jnp.arange(8)
    faces = (
        (lower_x, below_x, upper_x, above_x, 2),
        (lower_y, below_y, upper_y, above_y, 3),
        (lower_z, outer_lower_z, upper_z, outer_upper_z, 4),
    )
    for direction, (low_in, low_out, high_in, high_out, axis) in enumerate(faces):
        shape = [1, 1, 1, 1, 1]
        shape[axis] = 8
        place = node.reshape(shape)
        low_corr = jnp.expand_dims(face_correction(low_in, low_out, -1.0, direction + 1), axis)
        high_corr = jnp.expand_dims(face_correction(high_in, high_out, 1.0, direction + 1), axis)
        added = jnp.where(place == 0, low_corr, jnp.where(place == 7, high_corr, 0.0))
        result = result + added
    return result


def runge_kutta(fields, forcing):
    tables = kron_tables()
    step = lambda f: tendency(f, forcing, None, tables)
    section_one = fields + TIME_STEP * step(fields)
    section_two = 0.75 * fields + 0.25 * (section_one + TIME_STEP * step(section_one))
    return 1.0 / 3.0 * fields + 2.0 / 3.0 * (section_two + TIME_STEP * step(section_two))


def pick_rows(index, table):
    levels = jnp.arange(table.shape[0], dtype=jnp.int32)
    chosen = jnp.where(index[:, None, None] == levels[None, :, None], table[None], 0.0)
    return jnp.sum(chosen, axis=1)


def on_device(velocity, eddy_viscosity, cell_owner, cell_element, cell_position, acoustic_state):
    sources = source_cells(velocity, eddy_viscosity)
    cell_count = sources.shape[1] * sources.shape[2] * sources.shape[3]
    flat_source = sources.reshape(3, cell_count).astype(jnp.float32)
    owners = cell_owner.reshape(cell_count)
    elements = cell_element.reshape(cell_count)
    positions = cell_position.reshape(cell_count)
    owner_count = lax.axis_size("gx")
    capacity = 3 * cell_count // (2 * owner_count)
    owner_hot = (owners[:, None] == jnp.arange(owner_count, dtype=jnp.int32)[None, :]).astype(
        jnp.int32
    )
    earlier = jnp.cumsum(owner_hot, axis=0) - owner_hot
    order_within = jnp.sum(earlier * owner_hot, axis=1)
    slot_index = owners * capacity + order_within
    subcells = SUB * SUB * SUB
    ident = (elements * subcells + positions).astype(jnp.float32)
    payload = jnp.concatenate([flat_source, ident[None]], axis=0)
    send = (
        jnp.zeros((4, owner_count * capacity), jnp.float32)
        .at[:, slot_index]
        .set(payload)
        .reshape(4, owner_count, capacity)
    )
    send = jnp.transpose(send, (1, 0, 2)).reshape(owner_count, 4 * capacity)
    got = lax.all_to_all(send, "gx", split_axis=0, concat_axis=0, tiled=True)
    got = jnp.transpose(got.reshape(owner_count, 4, capacity), (1, 0, 2)).reshape(
        4, owner_count * capacity
    )
    got_source = got[:3].astype(jnp.bfloat16)
    got_ident = got[3].astype(jnp.int32)
    got_element = got_ident // subcells
    got_position = got_ident % subcells

    values = jnp.asarray(basis_table())
    along_a = pick_rows(got_position // (SUB * SUB), values)
    along_b = pick_rows(got_position // SUB % SUB, values)
    along_c = pick_rows(got_position % SUB, values)
    node_rows = (
        along_a[:, :, None, None] * along_b[:, None, :, None] * along_c[:, None, None, :]
    ).reshape(-1, NODES).astype(jnp.bfloat16)

    local_elems = acoustic_state.shape[1] * acoustic_state.shape[2] * acoustic_state.shape[3]
    element_hot = got_element[None, :] == jnp.arange(local_elems, dtype=jnp.int32)[:, None]
    weighted = jnp.where(element_hot[None], got_source[:, None, :], jnp.zeros((), jnp.bfloat16))
    weighted = weighted.reshape(3 * local_elems, -1)
    totals = jnp.dot(weighted, node_rows, preferred_element_type=jnp.float32)
    forcing = (totals * MOMENT_WEIGHT).reshape(3, local_elems, NODES)
    moments = jnp.moveaxis(forcing, 0, 1).reshape(
        acoustic_state.shape[1:4] + (3, NODES)
    )

    fields = acoustic_state.reshape(4, local_elems, 8, 8, 8)
    next_state = runge_kutta(fields, forcing).reshape(acoustic_state.shape)
    return (moments, next_state)


def solution(mesh):
    in_specs = (
        P(None, "gx", "gy", "gz"),
        P("gx", "gy", "gz"),
        P("gy", "gz", "gx", None),
        P("gy", "gz", "gx"),
        P("gy", "gz", "gx"),
        P(None, "gx", "gy", "gz", None),
    )
    out_specs = (P("gx", "gy", "gz", None, None), P(None, "gx", "gy", "gz", None))
    return jax.shard_map(
        on_device, mesh=mesh, in_specs=in_specs, out_specs=out_specs, check_vma=False
    )
```

```python
import jax
import jax.numpy as jnp
import numpy as np
from jax import lax
from jax.sharding import PartitionSpec as P

SUB = 16
NODES = 512


GLL_POINTS = np.array(
    [
        -1.0,
        -0.8717401485096066,
        -0.5917001814331423,
        -0.2092992179024789,
        0.2092992179024789,
        0.5917001814331423,
        0.8717401485096066,
        1.0,
    ]
)
LIFT_FACTOR = 28.0
TIME_STEP = 0.01
COUPLING = 4.0
MOMENT_WEIGHT = 0.0625


def derivative_matrix():
    points = GLL_POINTS
    barycentric = np.ones(8)
    for j in range(8):
        for m in range(8):
            if m != j:
                barycentric[j] = barycentric[j] / (points[j] - points[m])
    matrix = np.zeros((8, 8))
    for i in range(8):
        for j in range(8):
            if i != j:
                matrix[i, j] = barycentric[j] / barycentric[i] / (points[i] - points[j])
        matrix[i, i] = -np.sum(matrix[i])
    return matrix


def kron_tables():
    matrix = derivative_matrix().T
    node = np.arange(NODES)
    spreads = [matrix[:, node // 64], matrix[:, node // 8 % 8], matrix[:, node % 8]]
    spreads = lax.optimization_barrier([jnp.asarray(t, jnp.float32) for t in spreads])
    row = lax.broadcasted_iota(jnp.int32, (NODES, NODES), 0)
    col = lax.broadcasted_iota(jnp.int32, (NODES, NODES), 1)
    same_a = row // 64 == col // 64
    same_b = row // 8 % 8 == col // 8 % 8
    same_c = row % 8 == col % 8
    shape = (8, 8, 8, NODES)
    along_x = jnp.broadcast_to(spreads[0][:, None, None, :], shape).reshape(NODES, NODES)
    along_y = jnp.broadcast_to(spreads[1][None, :, None, :], shape).reshape(NODES, NODES)
    along_z = jnp.broadcast_to(spreads[2][None, None, :, :], shape).reshape(NODES, NODES)
    zero = jnp.zeros((), jnp.float32)
    return [
        jnp.where(same_b & same_c, along_x, zero),
        jnp.where(same_a & same_c, along_y, zero),
        jnp.where(same_a & same_b, along_z, zero),
    ]


def basis_table():
    points = GLL_POINTS
    centres = -1.0 + (2.0 * np.arange(SUB) + 1.0) / SUB
    values = np.ones((SUB, 8))
    for j in range(8):
        for m in range(8):
            if m != j:
                values[:, j] = values[:, j] * (centres - points[m]) / (points[j] - points[m])
    return np.asarray(values, dtype=np.float32)


def neighbours(lower, upper, axis):
    count = lax.axis_size(axis)
    if count == 1:
        return jnp.zeros_like(upper), jnp.zeros_like(lower)
    if count == 2:
        index = lax.axis_index(axis)
        sent = jnp.where(index == 0, upper, lower)
        got = lax.ppermute(sent, axis, [(0, 1), (1, 0)])
        zero = jnp.zeros_like(got)
        return jnp.where(index == 1, got, zero), jnp.where(index == 0, got, zero)
    from_below = lax.ppermute(upper, axis, [(i, i + 1) for i in range(count - 1)])
    from_above = lax.ppermute(lower, axis, [(i + 1, i) for i in range(count - 1)])
    return from_below, from_above


def source_cells(velocity, viscosity):
    below_x, above_x = neighbours(velocity[:, :1], velocity[:, -1:], "gx")
    below_y, above_y = neighbours(velocity[:, :, :1], velocity[:, :, -1:], "gy")
    below_z, above_z = neighbours(velocity[..., :1], velocity[..., -1:], "gz")
    centre = velocity.astype(jnp.float32)
    f32 = lambda t: t.astype(jnp.float32)
    plus_x = jnp.concatenate([centre[:, 1:], f32(above_x)], axis=1)
    minus_x = jnp.concatenate([f32(below_x), centre[:, :-1]], axis=1)
    plus_y = jnp.concatenate([centre[:, :, 1:], f32(above_y)], axis=2)
    minus_y = jnp.concatenate([f32(below_y), centre[:, :, :-1]], axis=2)
    plus_z = jnp.concatenate([centre[..., 1:], f32(above_z)], axis=3)
    minus_z = jnp.concatenate([f32(below_z), centre[..., :-1]], axis=3)
    grad_x = 0.5 * (plus_x - minus_x)
    grad_y = 0.5 * (plus_y - minus_y)
    grad_z = 0.5 * (plus_z - minus_z)
    laplace = plus_x + minus_x + plus_y + minus_y + plus_z + minus_z - 6.0 * centre
    curl_x = grad_y[2] - grad_z[1]
    curl_y = grad_z[0] - grad_x[2]
    curl_z = grad_x[1] - grad_y[0]
    lamb_x = curl_y * centre[2] - curl_z * centre[1]
    lamb_y = curl_z * centre[0] - curl_x * centre[2]
    lamb_z = curl_x * centre[1] - curl_y * centre[0]
    lamb = jnp.stack([lamb_x, lamb_y, lamb_z])
    return (viscosity[None] * laplace - lamb).astype(jnp.bfloat16)


def face_correction(inside, outside, normal, component):
    difference = inside - outside
    result = -0.5 * difference
    first = result[0] + 0.5 * normal * difference[component]
    chosen = result[component] + 0.5 * normal * difference[0]
    parts = [result[i] for i in range(4)]
    parts[0] = first
    parts[component] = chosen
    return LIFT_FACTOR * jnp.stack(parts)


def tendency(fields, forcing, tables):
    highest = lax.Precision.HIGHEST
    count = fields.shape[1]
    grads = [jnp.dot(fields[0], table, precision=highest) for table in tables]
    divergence = (
        jnp.dot(fields[1], tables[0], precision=highest)
        + jnp.dot(fields[2], tables[1], precision=highest)
        + jnp.dot(fields[3], tables[2], precision=highest)
    )
    result = jnp.stack(
        [
            -divergence,
            COUPLING * forcing[0] - grads[0],
            COUPLING * forcing[1] - grads[1],
            COUPLING * forcing[2] - grads[2],
        ]
    )

    face = 64
    below_x, above_x = neighbours(fields[..., :face], fields[..., NODES - face :], "gx")
    outer_lower_x = jnp.pad(below_x, ((0, 0), (0, 0), (0, NODES - face)))
    outer_upper_x = jnp.pad(above_x, ((0, 0), (0, 0), (NODES - face, 0)))
    below_y, above_y = neighbours(fields, fields, "gy")
    outer_lower_y = jnp.roll(below_y, -56, axis=2)
    outer_upper_y = jnp.roll(above_y, 56, axis=2)
    below_z, above_z = neighbours(fields[:, :1], fields[:, count - 1 :], "gz")
    outer_lower_z = jnp.roll(jnp.concatenate([below_z, fields[:, :-1]], axis=1), -7, axis=2)
    outer_upper_z = jnp.roll(jnp.concatenate([fields[:, 1:], above_z], axis=1), 7, axis=2)

    node = jnp.arange(NODES, dtype=jnp.int32)
    places = (node // 64, node // 8 % 8, node % 8)
    faces = (
        (outer_lower_x, outer_upper_x),
        (outer_lower_y, outer_upper_y),
        (outer_lower_z, outer_upper_z),
    )
    for direction, (low_out, high_out) in enumerate(faces):
        place = places[direction]
        low_corr = face_correction(fields, low_out, -1.0, direction + 1)
        high_corr = face_correction(fields, high_out, 1.0, direction + 1)
        added = jnp.where(place == 0, low_corr, jnp.where(place == 7, high_corr, 0.0))
        result = result + added
    return result


def runge_kutta(fields, forcing):
    tables = kron_tables()
    step = lambda f: tendency(f, forcing, tables)
    section_one = fields + TIME_STEP * step(fields)
    section_two = 0.75 * fields + 0.25 * (section_one + TIME_STEP * step(section_one))
    return 1.0 / 3.0 * fields + 2.0 / 3.0 * (section_two + TIME_STEP * step(section_two))


def pick_columns(index, table):
    levels = jnp.arange(table.shape[1], dtype=jnp.int32)
    chosen = jnp.where(index[None, None, :] == levels[None, :, None], table[:, :, None], 0.0)
    return jnp.sum(chosen, axis=1)


def on_device(velocity, eddy_viscosity, cell_owner, cell_element, cell_position, acoustic_state):
    sources = source_cells(velocity, eddy_viscosity)
    cell_count = sources.shape[1] * sources.shape[2] * sources.shape[3]
    flat_source = sources.reshape(3, cell_count).astype(jnp.float32)
    owners = cell_owner.reshape(cell_count)
    elements = cell_element.reshape(cell_count)
    positions = cell_position.reshape(cell_count)
    owner_count = lax.axis_size("gx")
    capacity = 3 * cell_count // (2 * owner_count)
    owner_hot = (owners[:, None] == jnp.arange(owner_count, dtype=jnp.int32)[None, :]).astype(
        jnp.int32
    )
    earlier = jnp.cumsum(owner_hot, axis=0) - owner_hot
    order_within = jnp.sum(earlier * owner_hot, axis=1)
    slot_index = owners * capacity + order_within
    subcells = SUB * SUB * SUB
    ident = (elements * subcells + positions).astype(jnp.float32)
    payload = jnp.concatenate([flat_source, ident[None]], axis=0)
    send = (
        jnp.zeros((4, owner_count * capacity), jnp.float32)
        .at[:, slot_index]
        .set(payload)
        .reshape(4, owner_count, capacity)
    )
    send = jnp.transpose(send, (1, 0, 2)).reshape(owner_count, 4 * capacity)
    got = lax.all_to_all(send, "gx", split_axis=0, concat_axis=0, tiled=True)
    got = jnp.transpose(got.reshape(owner_count, 4, capacity), (1, 0, 2)).reshape(
        4, owner_count * capacity
    )
    got_source = got[:3].astype(jnp.bfloat16)
    got_ident = got[3].astype(jnp.int32)
    got_element = got_ident // subcells
    got_position = got_ident % subcells

    values = jnp.asarray(basis_table().T)
    along_a = pick_columns(got_position // (SUB * SUB), values)
    along_b = pick_columns(got_position // SUB % SUB, values)
    along_c = pick_columns(got_position % SUB, values)
    rows = got_position.shape[0]
    node_columns = (
        along_a[:, None, None, :] * along_b[None, :, None, :] * along_c[None, None, :, :]
    ).reshape(NODES, rows).astype(jnp.bfloat16)

    local_elems = acoustic_state.shape[1] * acoustic_state.shape[2] * acoustic_state.shape[3]
    element_hot = got_element[None, :] == jnp.arange(local_elems, dtype=jnp.int32)[:, None]
    weighted = jnp.where(element_hot[None], got_source[:, None, :], jnp.zeros((), jnp.bfloat16))
    weighted = weighted.reshape(3 * local_elems, rows)
    totals = lax.dot_general(
        weighted, node_columns, (((1,), (1,)), ((), ())), preferred_element_type=jnp.float32
    )
    forcing = (totals * MOMENT_WEIGHT).reshape(3, local_elems, NODES)
    moments = jnp.moveaxis(forcing, 0, 1).reshape(
        acoustic_state.shape[1:4] + (3, NODES)
    )

    fields = acoustic_state.reshape(4, local_elems, NODES)
    next_state = runge_kutta(fields, forcing).reshape(acoustic_state.shape)
    return (moments, next_state)


def solution(mesh):
    in_specs = (
        P(None, "gx", "gy", "gz"),
        P("gx", "gy", "gz"),
        P("gy", "gz", "gx", None),
        P("gy", "gz", "gx"),
        P("gy", "gz", "gx"),
        P(None, "gx", "gy", "gz", None),
    )
    out_specs = (P("gx", "gy", "gz", None, None), P(None, "gx", "gy", "gz", None))
    return jax.shard_map(
        on_device, mesh=mesh, in_specs=in_specs, out_specs=out_specs, check_vma=False
    )
```

```python
import jax
import jax.numpy as jnp
import numpy as np
from jax import lax
from jax.sharding import PartitionSpec as P

SUB = 16
NODES = 512


GLL_POINTS = np.array(
    [
        -1.0,
        -0.8717401485096066,
        -0.5917001814331423,
        -0.2092992179024789,
        0.2092992179024789,
        0.5917001814331423,
        0.8717401485096066,
        1.0,
    ]
)
LIFT_FACTOR = 28.0
TIME_STEP = 0.01
COUPLING = 4.0
MOMENT_WEIGHT = 0.0625


def derivative_matrix():
    points = GLL_POINTS
    barycentric = np.ones(8)
    for j in range(8):
        for m in range(8):
            if m != j:
                barycentric[j] = barycentric[j] / (points[j] - points[m])
    matrix = np.zeros((8, 8))
    for i in range(8):
        for j in range(8):
            if i != j:
                matrix[i, j] = barycentric[j] / barycentric[i] / (points[i] - points[j])
        matrix[i, i] = -np.sum(matrix[i])
    return matrix


def kron_tables():
    matrix = derivative_matrix().T
    node = np.arange(NODES)
    spreads = [matrix[:, node // 64], matrix[:, node // 8 % 8], matrix[:, node % 8]]
    spreads = lax.optimization_barrier([jnp.asarray(t, jnp.float32) for t in spreads])
    row = lax.broadcasted_iota(jnp.int32, (NODES, NODES), 0)
    col = lax.broadcasted_iota(jnp.int32, (NODES, NODES), 1)
    same_a = row // 64 == col // 64
    same_b = row // 8 % 8 == col // 8 % 8
    same_c = row % 8 == col % 8
    shape = (8, 8, 8, NODES)
    along_x = jnp.broadcast_to(spreads[0][:, None, None, :], shape).reshape(NODES, NODES)
    along_y = jnp.broadcast_to(spreads[1][None, :, None, :], shape).reshape(NODES, NODES)
    along_z = jnp.broadcast_to(spreads[2][None, None, :, :], shape).reshape(NODES, NODES)
    zero = jnp.zeros((), jnp.float32)
    return [
        jnp.where(same_b & same_c, along_x, zero),
        jnp.where(same_a & same_c, along_y, zero),
        jnp.where(same_a & same_b, along_z, zero),
    ]


def basis_table():
    points = GLL_POINTS
    centres = -1.0 + (2.0 * np.arange(SUB) + 1.0) / SUB
    values = np.ones((SUB, 8))
    for j in range(8):
        for m in range(8):
            if m != j:
                values[:, j] = values[:, j] * (centres - points[m]) / (points[j] - points[m])
    return np.asarray(values, dtype=np.float32)


def neighbours(lower, upper, axis):
    count = lax.axis_size(axis)
    if count == 1:
        return jnp.zeros_like(upper), jnp.zeros_like(lower)
    if count == 2:
        index = lax.axis_index(axis)
        sent = jnp.where(index == 0, upper, lower)
        got = lax.ppermute(sent, axis, [(0, 1), (1, 0)])
        zero = jnp.zeros_like(got)
        return jnp.where(index == 1, got, zero), jnp.where(index == 0, got, zero)
    from_below = lax.ppermute(upper, axis, [(i, i + 1) for i in range(count - 1)])
    from_above = lax.ppermute(lower, axis, [(i + 1, i) for i in range(count - 1)])
    return from_below, from_above


def neighbours_joined(pairs, axis):
    flat = lambda t: t.astype(jnp.float32).reshape(-1)
    lower = jnp.concatenate([flat(low) for low, _ in pairs])
    upper = jnp.concatenate([flat(high) for _, high in pairs])
    from_below, from_above = neighbours(lower, upper, axis)
    results = []
    start = 0
    for low, high in pairs:
        size = low.size
        results.append(
            (
                from_below[start : start + size].reshape(high.shape).astype(high.dtype),
                from_above[start : start + size].reshape(low.shape).astype(low.dtype),
            )
        )
        start += size
    return results


def velocity_faces(velocity):
    return (
        (velocity[:, :1], velocity[:, -1:]),
        (velocity[:, :, :1], velocity[:, :, -1:]),
        (velocity[..., :1], velocity[..., -1:]),
    )


def state_faces(fields):
    count = fields.shape[1]
    face = 64
    return (
        (fields[..., :face], fields[..., NODES - face :]),
        (fields, fields),
        (fields[:, :1], fields[:, count - 1 :]),
    )


def exchange(face_sets):
    per_axis = []
    for direction, axis in enumerate(("gx", "gy", "gz")):
        per_axis.append(neighbours_joined([faces[direction] for faces in face_sets], axis))
    return [tuple(per_axis[d][k] for d in range(3)) for k in range(len(face_sets))]


def source_cells(velocity, viscosity, halo):
    (below_x, above_x), (below_y, above_y), (below_z, above_z) = halo
    centre = velocity.astype(jnp.float32)
    f32 = lambda t: t.astype(jnp.float32)
    plus_x = jnp.concatenate([centre[:, 1:], f32(above_x)], axis=1)
    minus_x = jnp.concatenate([f32(below_x), centre[:, :-1]], axis=1)
    plus_y = jnp.concatenate([centre[:, :, 1:], f32(above_y)], axis=2)
    minus_y = jnp.concatenate([f32(below_y), centre[:, :, :-1]], axis=2)
    plus_z = jnp.concatenate([centre[..., 1:], f32(above_z)], axis=3)
    minus_z = jnp.concatenate([f32(below_z), centre[..., :-1]], axis=3)
    grad_x = 0.5 * (plus_x - minus_x)
    grad_y = 0.5 * (plus_y - minus_y)
    grad_z = 0.5 * (plus_z - minus_z)
    laplace = plus_x + minus_x + plus_y + minus_y + plus_z + minus_z - 6.0 * centre
    curl_x = grad_y[2] - grad_z[1]
    curl_y = grad_z[0] - grad_x[2]
    curl_z = grad_x[1] - grad_y[0]
    lamb_x = curl_y * centre[2] - curl_z * centre[1]
    lamb_y = curl_z * centre[0] - curl_x * centre[2]
    lamb_z = curl_x * centre[1] - curl_y * centre[0]
    lamb = jnp.stack([lamb_x, lamb_y, lamb_z])
    return (viscosity[None] * laplace - lamb).astype(jnp.bfloat16)


def face_correction(inside, outside, normal, component):
    difference = inside - outside
    result = -0.5 * difference
    first = result[0] + 0.5 * normal * difference[component]
    chosen = result[component] + 0.5 * normal * difference[0]
    parts = [result[i] for i in range(4)]
    parts[0] = first
    parts[component] = chosen
    return LIFT_FACTOR * jnp.stack(parts)


def tendency(fields, forcing, tables, halo=None):
    highest = lax.Precision.HIGHEST
    count = fields.shape[1]
    grads = [jnp.dot(fields[0], table, precision=highest) for table in tables]
    divergence = (
        jnp.dot(fields[1], tables[0], precision=highest)
        + jnp.dot(fields[2], tables[1], precision=highest)
        + jnp.dot(fields[3], tables[2], precision=highest)
    )
    result = jnp.stack(
        [
            -divergence,
            COUPLING * forcing[0] - grads[0],
            COUPLING * forcing[1] - grads[1],
            COUPLING * forcing[2] - grads[2],
        ]
    )

    face = 64
    if halo is None:
        halo = exchange([state_faces(fields)])[0]
    (below_x, above_x), (below_y, above_y), (below_z, above_z) = halo
    outer_lower_x = jnp.pad(below_x, ((0, 0), (0, 0), (0, NODES - face)))
    outer_upper_x = jnp.pad(above_x, ((0, 0), (0, 0), (NODES - face, 0)))
    outer_lower_y = jnp.roll(below_y, -56, axis=2)
    outer_upper_y = jnp.roll(above_y, 56, axis=2)
    outer_lower_z = jnp.roll(jnp.concatenate([below_z, fields[:, :-1]], axis=1), -7, axis=2)
    outer_upper_z = jnp.roll(jnp.concatenate([fields[:, 1:], above_z], axis=1), 7, axis=2)

    node = jnp.arange(NODES, dtype=jnp.int32)
    places = (node // 64, node // 8 % 8, node % 8)
    faces = (
        (outer_lower_x, outer_upper_x),
        (outer_lower_y, outer_upper_y),
        (outer_lower_z, outer_upper_z),
    )
    for direction, (low_out, high_out) in enumerate(faces):
        place = places[direction]
        low_corr = face_correction(fields, low_out, -1.0, direction + 1)
        high_corr = face_correction(fields, high_out, 1.0, direction + 1)
        added = jnp.where(place == 0, low_corr, jnp.where(place == 7, high_corr, 0.0))
        result = result + added
    return result


def runge_kutta(fields, forcing, halo):
    tables = kron_tables()
    step = lambda f: tendency(f, forcing, tables)
    section_one = fields + TIME_STEP * tendency(fields, forcing, tables, halo)
    section_two = 0.75 * fields + 0.25 * (section_one + TIME_STEP * step(section_one))
    return 1.0 / 3.0 * fields + 2.0 / 3.0 * (section_two + TIME_STEP * step(section_two))


def pick_columns(index, table):
    levels = jnp.arange(table.shape[1], dtype=jnp.int32)
    chosen = jnp.where(index[None, None, :] == levels[None, :, None], table[:, :, None], 0.0)
    return jnp.sum(chosen, axis=1)


def on_device(velocity, eddy_viscosity, cell_owner, cell_element, cell_position, acoustic_state):
    local_elems = acoustic_state.shape[1] * acoustic_state.shape[2] * acoustic_state.shape[3]
    fields = acoustic_state.reshape(4, local_elems, NODES)
    velocity_halo, state_halo = exchange([velocity_faces(velocity), state_faces(fields)])
    sources = source_cells(velocity, eddy_viscosity, velocity_halo)
    cell_count = sources.shape[1] * sources.shape[2] * sources.shape[3]
    flat_source = sources.reshape(3, cell_count).astype(jnp.float32)
    owners = cell_owner.reshape(cell_count)
    elements = cell_element.reshape(cell_count)
    positions = cell_position.reshape(cell_count)
    owner_count = lax.axis_size("gx")
    capacity = 3 * cell_count // (2 * owner_count)
    owner_hot = (owners[:, None] == jnp.arange(owner_count, dtype=jnp.int32)[None, :]).astype(
        jnp.int32
    )
    earlier = jnp.cumsum(owner_hot, axis=0) - owner_hot
    order_within = jnp.sum(earlier * owner_hot, axis=1)
    slot_index = owners * capacity + order_within
    subcells = SUB * SUB * SUB
    ident = (elements * subcells + positions).astype(jnp.float32)
    payload = jnp.concatenate([flat_source, ident[None]], axis=0)
    send = (
        jnp.zeros((4, owner_count * capacity), jnp.float32)
        .at[:, slot_index]
        .set(payload)
        .reshape(4, owner_count, capacity)
    )
    got = lax.all_to_all(send, "gx", split_axis=1, concat_axis=1, tiled=True)
    got = got.reshape(4, owner_count * capacity)
    got_source = got[:3].astype(jnp.bfloat16)
    got_ident = got[3].astype(jnp.int32)
    got_element = got_ident // subcells
    got_position = got_ident % subcells

    values = jnp.asarray(basis_table().T)
    along_a = pick_columns(got_position // (SUB * SUB), values)
    along_b = pick_columns(got_position // SUB % SUB, values)
    along_c = pick_columns(got_position % SUB, values)
    rows = got_position.shape[0]
    node_columns = (
        along_a[:, None, None, :] * along_b[None, :, None, :] * along_c[None, None, :, :]
    ).reshape(NODES, rows).astype(jnp.bfloat16)

    element_hot = got_element[None, :] == jnp.arange(local_elems, dtype=jnp.int32)[:, None]
    weighted = jnp.where(element_hot[None], got_source[:, None, :], jnp.zeros((), jnp.bfloat16))
    weighted = weighted.reshape(3 * local_elems, rows)
    totals = lax.dot_general(
        weighted, node_columns, (((1,), (1,)), ((), ())), preferred_element_type=jnp.float32
    )
    forcing = (totals * MOMENT_WEIGHT).reshape(3, local_elems, NODES)
    moments = jnp.moveaxis(forcing, 0, 1).reshape(
        acoustic_state.shape[1:4] + (3, NODES)
    )

    next_state = runge_kutta(fields, forcing, state_halo).reshape(acoustic_state.shape)
    return (moments, next_state)


def solution(mesh):
    in_specs = (
        P(None, "gx", "gy", "gz"),
        P("gx", "gy", "gz"),
        P("gy", "gz", "gx", None),
        P("gy", "gz", "gx"),
        P("gy", "gz", "gx"),
        P(None, "gx", "gy", "gz", None),
    )
    out_specs = (P("gx", "gy", "gz", None, None), P(None, "gx", "gy", "gz", None))
    return jax.shard_map(
        on_device, mesh=mesh, in_specs=in_specs, out_specs=out_specs, check_vma=False
    )
```

```python
import jax
import jax.numpy as jnp
import numpy as np
from jax import lax
from jax.sharding import PartitionSpec as P


SUB = 16
NODES = 512


GLL_POINTS = np.array(
    [
        -1.0,
        -0.8717401485096066,
        -0.5917001814331423,
        -0.2092992179024789,
        0.2092992179024789,
        0.5917001814331423,
        0.8717401485096066,
        1.0,
    ]
)
LIFT_FACTOR = 28.0
TIME_STEP = 0.01
COUPLING = 4.0
MOMENT_WEIGHT = 0.0625


def derivative_matrix():
    points = GLL_POINTS
    barycentric = np.ones(8)
    for j in range(8):
        for m in range(8):
            if m != j:
                barycentric[j] = barycentric[j] / (points[j] - points[m])
    matrix = np.zeros((8, 8))
    for i in range(8):
        for j in range(8):
            if i != j:
                matrix[i, j] = barycentric[j] / barycentric[i] / (points[i] - points[j])
        matrix[i, i] = -np.sum(matrix[i])
    return matrix


def kron_tables():
    matrix = derivative_matrix().T
    node = np.arange(NODES)
    spreads = [matrix[:, node // 64], matrix[:, node // 8 % 8], matrix[:, node % 8]]
    spreads = lax.optimization_barrier([jnp.asarray(t, jnp.float32) for t in spreads])
    row = lax.broadcasted_iota(jnp.int32, (NODES, NODES), 0)
    col = lax.broadcasted_iota(jnp.int32, (NODES, NODES), 1)
    same_a = row // 64 == col // 64
    same_b = row // 8 % 8 == col // 8 % 8
    same_c = row % 8 == col % 8
    shape = (8, 8, 8, NODES)
    along_x = jnp.broadcast_to(spreads[0][:, None, None, :], shape).reshape(NODES, NODES)
    along_y = jnp.broadcast_to(spreads[1][None, :, None, :], shape).reshape(NODES, NODES)
    along_z = jnp.broadcast_to(spreads[2][None, None, :, :], shape).reshape(NODES, NODES)
    zero = jnp.zeros((), jnp.float32)
    return [
        jnp.where(same_b & same_c, along_x, zero),
        jnp.where(same_a & same_c, along_y, zero),
        jnp.where(same_a & same_b, along_z, zero),
    ]


def basis_table():
    points = GLL_POINTS
    centres = -1.0 + (2.0 * np.arange(SUB) + 1.0) / SUB
    values = np.ones((SUB, 8))
    for j in range(8):
        for m in range(8):
            if m != j:
                values[:, j] = values[:, j] * (centres - points[m]) / (points[j] - points[m])
    return np.asarray(values, dtype=np.float32)


def neighbours(lower, upper, axis):
    count = lax.axis_size(axis)
    if count == 1:
        return jnp.zeros_like(upper), jnp.zeros_like(lower)
    if count == 2:
        index = lax.axis_index(axis)
        sent = jnp.where(index == 0, upper, lower)
        got = lax.ppermute(sent, axis, [(0, 1), (1, 0)])
        zero = jnp.zeros_like(got)
        return jnp.where(index == 1, got, zero), jnp.where(index == 0, got, zero)
    from_below = lax.ppermute(upper, axis, [(i, i + 1) for i in range(count - 1)])
    from_above = lax.ppermute(lower, axis, [(i + 1, i) for i in range(count - 1)])
    return from_below, from_above


def source_cells(velocity, viscosity):
    below_x, above_x = neighbours(velocity[:, :1], velocity[:, -1:], "gx")
    below_y, above_y = neighbours(velocity[:, :, :1], velocity[:, :, -1:], "gy")
    below_z, above_z = neighbours(velocity[..., :1], velocity[..., -1:], "gz")
    centre = velocity.astype(jnp.float32)
    f32 = lambda t: t.astype(jnp.float32)
    plus_x = jnp.concatenate([centre[:, 1:], f32(above_x)], axis=1)
    minus_x = jnp.concatenate([f32(below_x), centre[:, :-1]], axis=1)
    plus_y = jnp.concatenate([centre[:, :, 1:], f32(above_y)], axis=2)
    minus_y = jnp.concatenate([f32(below_y), centre[:, :, :-1]], axis=2)
    plus_z = jnp.concatenate([centre[..., 1:], f32(above_z)], axis=3)
    minus_z = jnp.concatenate([f32(below_z), centre[..., :-1]], axis=3)
    grad_x = 0.5 * (plus_x - minus_x)
    grad_y = 0.5 * (plus_y - minus_y)
    grad_z = 0.5 * (plus_z - minus_z)
    laplace = plus_x + minus_x + plus_y + minus_y + plus_z + minus_z - 6.0 * centre
    curl_x = grad_y[2] - grad_z[1]
    curl_y = grad_z[0] - grad_x[2]
    curl_z = grad_x[1] - grad_y[0]
    lamb_x = curl_y * centre[2] - curl_z * centre[1]
    lamb_y = curl_z * centre[0] - curl_x * centre[2]
    lamb_z = curl_x * centre[1] - curl_y * centre[0]
    lamb = jnp.stack([lamb_x, lamb_y, lamb_z])
    return (viscosity[None] * laplace - lamb).astype(jnp.bfloat16)


def face_correction(inside, outside, normal, component):
    difference = inside - outside
    result = -0.5 * difference
    first = result[0] + 0.5 * normal * difference[component]
    chosen = result[component] + 0.5 * normal * difference[0]
    parts = [result[i] for i in range(4)]
    parts[0] = first
    parts[component] = chosen
    return LIFT_FACTOR * jnp.stack(parts)


def tendency(fields, forcing, tables):
    highest = lax.Precision.HIGHEST
    count = fields.shape[1]
    grads = [jnp.dot(fields[0], table, precision=highest) for table in tables]
    divergence = (
        jnp.dot(fields[1], tables[0], precision=highest)
        + jnp.dot(fields[2], tables[1], precision=highest)
        + jnp.dot(fields[3], tables[2], precision=highest)
    )
    result = jnp.stack(
        [
            -divergence,
            COUPLING * forcing[0] - grads[0],
            COUPLING * forcing[1] - grads[1],
            COUPLING * forcing[2] - grads[2],
        ]
    )

    face = 64
    below_x, above_x = neighbours(fields[..., :face], fields[..., NODES - face :], "gx")
    below_y, above_y = neighbours(fields, fields, "gy")
    below_z, above_z = neighbours(fields[:, :1], fields[:, count - 1 :], "gz")
    outer_lower_x = jnp.pad(below_x, ((0, 0), (0, 0), (0, NODES - face)))
    outer_upper_x = jnp.pad(above_x, ((0, 0), (0, 0), (NODES - face, 0)))
    outer_lower_y = jnp.roll(below_y, -56, axis=2)
    outer_upper_y = jnp.roll(above_y, 56, axis=2)
    outer_lower_z = jnp.roll(jnp.concatenate([below_z, fields[:, :-1]], axis=1), -7, axis=2)
    outer_upper_z = jnp.roll(jnp.concatenate([fields[:, 1:], above_z], axis=1), 7, axis=2)

    node = jnp.arange(NODES, dtype=jnp.int32)
    places = (node // 64, node // 8 % 8, node % 8)
    faces = (
        (outer_lower_x, outer_upper_x),
        (outer_lower_y, outer_upper_y),
        (outer_lower_z, outer_upper_z),
    )
    for direction, (low_out, high_out) in enumerate(faces):
        place = places[direction]
        low_corr = face_correction(fields, low_out, -1.0, direction + 1)
        high_corr = face_correction(fields, high_out, 1.0, direction + 1)
        added = jnp.where(place == 0, low_corr, jnp.where(place == 7, high_corr, 0.0))
        result = result + added
    return result


def runge_kutta(fields, forcing):
    tables = kron_tables()
    step = lambda f: tendency(f, forcing, tables)
    section_one = fields + TIME_STEP * tendency(fields, forcing, tables)
    section_two = 0.75 * fields + 0.25 * (section_one + TIME_STEP * step(section_one))
    return 1.0 / 3.0 * fields + 2.0 / 3.0 * (section_two + TIME_STEP * step(section_two))


def pick_columns(index, table):
    levels = jnp.arange(table.shape[1], dtype=jnp.int32)
    chosen = jnp.where(index[None, None, :] == levels[None, :, None], table[:, :, None], 0.0)
    return jnp.sum(chosen, axis=1)


def on_device_body(velocity, eddy_viscosity, cell_owner, cell_element, cell_position, acoustic_state):
    sources = source_cells(velocity, eddy_viscosity)
    cell_count = sources.shape[1] * sources.shape[2] * sources.shape[3]
    flat_source = sources.reshape(3, cell_count).astype(jnp.float32)
    owners = cell_owner.reshape(cell_count)
    elements = cell_element.reshape(cell_count)
    positions = cell_position.reshape(cell_count)
    owner_count = lax.axis_size("gx")
    capacity = 3 * cell_count // (2 * owner_count)
    owner_hot = (owners[:, None] == jnp.arange(owner_count, dtype=jnp.int32)[None, :]).astype(
        jnp.int32
    )
    earlier = jnp.cumsum(owner_hot, axis=0) - owner_hot
    order_within = jnp.sum(earlier * owner_hot, axis=1)
    slot_index = owners * capacity + order_within
    subcells = SUB * SUB * SUB
    ident = (elements * subcells + positions).astype(jnp.float32)
    payload = jnp.concatenate([flat_source, ident[None]], axis=0)
    send = (
        jnp.zeros((4, owner_count * capacity), jnp.float32)
        .at[:, slot_index]
        .set(payload)
        .reshape(4, owner_count, capacity)
    )
    send = jnp.transpose(send, (1, 0, 2)).reshape(owner_count, 4 * capacity)
    got = lax.all_to_all(send, "gx", split_axis=0, concat_axis=0, tiled=True)
    got = jnp.transpose(got.reshape(owner_count, 4, capacity), (1, 0, 2)).reshape(
        4, owner_count * capacity
    )
    got_source = got[:3].astype(jnp.bfloat16)
    got_ident = got[3].astype(jnp.int32)
    got_element = got_ident // subcells
    got_position = got_ident % subcells

    values = jnp.asarray(basis_table().T)
    along_a = pick_columns(got_position // (SUB * SUB), values)
    along_b = pick_columns(got_position // SUB % SUB, values)
    along_c = pick_columns(got_position % SUB, values)
    rows = got_position.shape[0]
    node_columns = (
        along_a[:, None, None, :] * along_b[None, :, None, :] * along_c[None, None, :, :]
    ).reshape(NODES, rows).astype(jnp.bfloat16)

    local_elems = acoustic_state.shape[1] * acoustic_state.shape[2] * acoustic_state.shape[3]
    element_hot = got_element[None, :] == jnp.arange(local_elems, dtype=jnp.int32)[:, None]
    weighted = jnp.where(element_hot[None], got_source[:, None, :], jnp.zeros((), jnp.bfloat16))
    weighted = weighted.reshape(3 * local_elems, rows)
    totals = lax.dot_general(
        weighted, node_columns, (((1,), (1,)), ((), ())), preferred_element_type=jnp.float32
    )
    forcing = (totals * MOMENT_WEIGHT).reshape(3, local_elems, NODES)
    moments = jnp.moveaxis(forcing, 0, 1).reshape(
        acoustic_state.shape[1:4] + (3, NODES)
    )

    fields = acoustic_state.reshape(4, local_elems, NODES)
    next_state = runge_kutta(fields, forcing).reshape(acoustic_state.shape)
    return (moments, next_state)


def solution(mesh):
    in_specs = (
        P(None, "gx", "gy", "gz"),
        P("gx", "gy", "gz"),
        P("gy", "gz", "gx", None),
        P("gy", "gz", "gx"),
        P("gy", "gz", "gx"),
        P(None, "gx", "gy", "gz", None),
    )
    out_specs = (P("gx", "gy", "gz", None, None), P(None, "gx", "gy", "gz", None))
    return jax.shard_map(
        on_device_body, mesh=mesh, in_specs=in_specs, out_specs=out_specs, check_vma=False
    )
```

```python
import jax
import jax.numpy as jnp
import numpy as np
from jax import lax
from jax.sharding import PartitionSpec as P


SUB = 16
NODES = 512


GLL_POINTS = np.array(
    [
        -1.0,
        -0.8717401485096066,
        -0.5917001814331423,
        -0.2092992179024789,
        0.2092992179024789,
        0.5917001814331423,
        0.8717401485096066,
        1.0,
    ]
)
LIFT_FACTOR = 28.0
TIME_STEP = 0.01
COUPLING = 4.0
MOMENT_WEIGHT = 0.0625


def derivative_matrix():
    points = GLL_POINTS
    barycentric = np.ones(8)
    for j in range(8):
        for m in range(8):
            if m != j:
                barycentric[j] = barycentric[j] / (points[j] - points[m])
    matrix = np.zeros((8, 8))
    for i in range(8):
        for j in range(8):
            if i != j:
                matrix[i, j] = barycentric[j] / barycentric[i] / (points[i] - points[j])
        matrix[i, i] = -np.sum(matrix[i])
    return matrix


def kron_tables():
    matrix = derivative_matrix().T
    node = np.arange(NODES)
    spreads = [matrix[:, node // 64], matrix[:, node // 8 % 8], matrix[:, node % 8]]
    spreads = lax.optimization_barrier([jnp.asarray(t, jnp.float32) for t in spreads])
    row = lax.broadcasted_iota(jnp.int32, (NODES, NODES), 0)
    col = lax.broadcasted_iota(jnp.int32, (NODES, NODES), 1)
    same_a = row // 64 == col // 64
    same_b = row // 8 % 8 == col // 8 % 8
    same_c = row % 8 == col % 8
    shape = (8, 8, 8, NODES)
    along_x = jnp.broadcast_to(spreads[0][:, None, None, :], shape).reshape(NODES, NODES)
    along_y = jnp.broadcast_to(spreads[1][None, :, None, :], shape).reshape(NODES, NODES)
    along_z = jnp.broadcast_to(spreads[2][None, None, :, :], shape).reshape(NODES, NODES)
    zero = jnp.zeros((), jnp.float32)
    return [
        jnp.where(same_b & same_c, along_x, zero),
        jnp.where(same_a & same_c, along_y, zero),
        jnp.where(same_a & same_b, along_z, zero),
    ]


def basis_table():
    points = GLL_POINTS
    centres = -1.0 + (2.0 * np.arange(SUB) + 1.0) / SUB
    values = np.ones((SUB, 8))
    for j in range(8):
        for m in range(8):
            if m != j:
                values[:, j] = values[:, j] * (centres - points[m]) / (points[j] - points[m])
    return np.asarray(values, dtype=np.float32)


def neighbours(lower, upper, axis):
    count = lax.axis_size(axis)
    if count == 1:
        return jnp.zeros_like(upper), jnp.zeros_like(lower)
    return neighbours_on(lower, upper, axis, count)


def neighbours_on(lower, upper, axis, count):
    if count == 2:
        index = lax.axis_index(axis)
        sent = jnp.where(index == 0, upper, lower)
        got = lax.ppermute(sent, axis, [(0, 1), (1, 0)])
        zero = jnp.zeros_like(got)
        return jnp.where(index == 1, got, zero), jnp.where(index == 0, got, zero)
    from_below = lax.ppermute(upper, axis, [(i, i + 1) for i in range(count - 1)])
    from_above = lax.ppermute(lower, axis, [(i + 1, i) for i in range(count - 1)])
    return from_below, from_above


def source_from_halo(velocity, viscosity):
    below_x, above_x = neighbours(velocity[:, :1], velocity[:, -1:], "gx")
    below_y, above_y = neighbours(velocity[:, :, :1], velocity[:, :, -1:], "gy")
    below_z, above_z = neighbours(velocity[..., :1], velocity[..., -1:], "gz")
    centre = velocity.astype(jnp.float32)
    f32 = lambda t: t.astype(jnp.float32)
    plus_x = jnp.concatenate([centre[:, 1:], f32(above_x)], axis=1)
    minus_x = jnp.concatenate([f32(below_x), centre[:, :-1]], axis=1)
    plus_y = jnp.concatenate([centre[:, :, 1:], f32(above_y)], axis=2)
    minus_y = jnp.concatenate([f32(below_y), centre[:, :, :-1]], axis=2)
    plus_z = jnp.concatenate([centre[..., 1:], f32(above_z)], axis=3)
    minus_z = jnp.concatenate([f32(below_z), centre[..., :-1]], axis=3)
    grad_x = 0.5 * (plus_x - minus_x)
    grad_y = 0.5 * (plus_y - minus_y)
    grad_z = 0.5 * (plus_z - minus_z)
    laplace = plus_x + minus_x + plus_y + minus_y + plus_z + minus_z - 6.0 * centre
    curl_x = grad_y[2] - grad_z[1]
    curl_y = grad_z[0] - grad_x[2]
    curl_z = grad_x[1] - grad_y[0]
    lamb_x = curl_y * centre[2] - curl_z * centre[1]
    lamb_y = curl_z * centre[0] - curl_x * centre[2]
    lamb_z = curl_x * centre[1] - curl_y * centre[0]
    lamb = jnp.stack([lamb_x, lamb_y, lamb_z])
    return (viscosity[None] * laplace - lamb).astype(jnp.bfloat16)


def face_correction(inside, outside, normal, component):
    difference = inside - outside
    result = -0.5 * difference
    first = result[0] + 0.5 * normal * difference[component]
    chosen = result[component] + 0.5 * normal * difference[0]
    parts = [result[i] for i in range(4)]
    parts[0] = first
    parts[component] = chosen
    return LIFT_FACTOR * jnp.stack(parts)


def tendency(fields, tables):
    highest = lax.Precision.HIGHEST
    count = fields.shape[1]
    grads = [jnp.dot(fields[0], table, precision=highest) for table in tables]
    divergence = (
        jnp.dot(fields[1], tables[0], precision=highest)
        + jnp.dot(fields[2], tables[1], precision=highest)
        + jnp.dot(fields[3], tables[2], precision=highest)
    )
    result = jnp.stack([-divergence, -grads[0], -grads[1], -grads[2]])

    face = 64
    below_x, above_x = neighbours(fields[..., :face], fields[..., NODES - face :], "gx")
    below_y, above_y = neighbours(fields, fields, "gy")
    below_z, above_z = neighbours(fields[:, :1], fields[:, count - 1 :], "gz")
    outer_lower_x = jnp.pad(below_x, ((0, 0), (0, 0), (0, NODES - face)))
    outer_upper_x = jnp.pad(above_x, ((0, 0), (0, 0), (NODES - face, 0)))
    outer_lower_y = jnp.roll(below_y, -56, axis=2)
    outer_upper_y = jnp.roll(above_y, 56, axis=2)
    outer_lower_z = jnp.roll(jnp.concatenate([below_z, fields[:, :-1]], axis=1), -7, axis=2)
    outer_upper_z = jnp.roll(jnp.concatenate([fields[:, 1:], above_z], axis=1), 7, axis=2)

    node = jnp.arange(NODES, dtype=jnp.int32)
    places = (node // 64, node // 8 % 8, node % 8)
    faces = (
        (outer_lower_x, outer_upper_x),
        (outer_lower_y, outer_upper_y),
        (outer_lower_z, outer_upper_z),
    )
    for direction, (low_out, high_out) in enumerate(faces):
        place = places[direction]
        low_corr = face_correction(fields, low_out, -1.0, direction + 1)
        high_corr = face_correction(fields, high_out, 1.0, direction + 1)
        added = jnp.where(place == 0, low_corr, jnp.where(place == 7, high_corr, 0.0))
        result = result + added
    return result


def runge_kutta(fields, forcing):
    tables = kron_tables()
    coupled = jnp.concatenate([jnp.zeros_like(forcing[:1]), COUPLING * forcing])
    step = lambda f: tendency(f, tables) + coupled
    first = tendency(fields, tables)
    section_one = fields + TIME_STEP * (first + coupled)
    section_two = 0.75 * fields + 0.25 * (section_one + TIME_STEP * step(section_one))
    return 1.0 / 3.0 * fields + 2.0 / 3.0 * (section_two + TIME_STEP * step(section_two))


def pick_columns(index, table):
    levels = jnp.arange(table.shape[1], dtype=jnp.int32)
    chosen = jnp.where(index[None, None, :] == levels[None, :, None], table[:, :, None], 0.0)
    return jnp.sum(chosen, axis=1)


def on_device_body(velocity, eddy_viscosity, cell_owner, cell_element, cell_position, acoustic_state):
    sources = source_from_halo(velocity, eddy_viscosity)
    cell_count = sources.shape[1] * sources.shape[2] * sources.shape[3]
    flat_source = sources.reshape(3, cell_count).astype(jnp.float32)
    owners = cell_owner.reshape(cell_count)
    elements = cell_element.reshape(cell_count)
    positions = cell_position.reshape(cell_count)
    owner_count = lax.axis_size("gx")
    capacity = 3 * cell_count // (2 * owner_count)
    owner_hot = (owners[:, None] == jnp.arange(owner_count, dtype=jnp.int32)[None, :]).astype(
        jnp.int32
    )
    earlier = jnp.cumsum(owner_hot, axis=0) - owner_hot
    order_within = jnp.sum(earlier * owner_hot, axis=1)
    slot_index = owners * capacity + order_within
    subcells = SUB * SUB * SUB
    ident = (elements * subcells + positions).astype(jnp.float32)
    payload = jnp.concatenate([flat_source, ident[None]], axis=0)
    send = (
        jnp.zeros((4, owner_count * capacity), jnp.float32)
        .at[:, slot_index]
        .set(payload)
        .reshape(4, owner_count, capacity)
    )
    send = jnp.transpose(send, (1, 0, 2)).reshape(owner_count, 4 * capacity)
    got = lax.all_to_all(send, "gx", split_axis=0, concat_axis=0, tiled=True)
    got = jnp.transpose(got.reshape(owner_count, 4, capacity), (1, 0, 2)).reshape(
        4, owner_count * capacity
    )
    got_source = got[:3].astype(jnp.bfloat16)
    got_ident = got[3].astype(jnp.int32)
    got_element = got_ident // subcells
    got_position = got_ident % subcells

    values = jnp.asarray(basis_table().T)
    along_a = pick_columns(got_position // (SUB * SUB), values)
    along_b = pick_columns(got_position // SUB % SUB, values)
    along_c = pick_columns(got_position % SUB, values)
    rows = got_position.shape[0]
    node_columns = (
        along_a[:, None, None, :] * along_b[None, :, None, :] * along_c[None, None, :, :]
    ).reshape(NODES, rows).astype(jnp.bfloat16)

    local_elems = acoustic_state.shape[1] * acoustic_state.shape[2] * acoustic_state.shape[3]
    element_hot = got_element[None, :] == jnp.arange(local_elems, dtype=jnp.int32)[:, None]
    weighted = jnp.where(element_hot[None], got_source[:, None, :], jnp.zeros((), jnp.bfloat16))
    weighted = weighted.reshape(3 * local_elems, rows)
    totals = lax.dot_general(
        weighted, node_columns, (((1,), (1,)), ((), ())), preferred_element_type=jnp.float32
    )
    forcing = (totals * MOMENT_WEIGHT).reshape(3, local_elems, NODES)
    moments = jnp.moveaxis(forcing, 0, 1).reshape(
        acoustic_state.shape[1:4] + (3, NODES)
    )

    fields = acoustic_state.reshape(4, local_elems, NODES)
    next_state = runge_kutta(fields, forcing).reshape(acoustic_state.shape)
    return (moments, next_state)


def solution(mesh):
    in_specs = (
        P(None, "gx", "gy", "gz"),
        P("gx", "gy", "gz"),
        P("gy", "gz", "gx", None),
        P("gy", "gz", "gx"),
        P("gy", "gz", "gx"),
        P(None, "gx", "gy", "gz", None),
    )
    out_specs = (P("gx", "gy", "gz", None, None), P(None, "gx", "gy", "gz", None))
    return jax.shard_map(
        on_device_body, mesh=mesh, in_specs=in_specs, out_specs=out_specs, check_vma=False
    )
```

```python
import jax
import jax.numpy as jnp
import numpy as np
from jax import lax
from jax.sharding import PartitionSpec as P


SUB = 16
NODES = 512


GLL_POINTS = np.array(
    [
        -1.0,
        -0.8717401485096066,
        -0.5917001814331423,
        -0.2092992179024789,
        0.2092992179024789,
        0.5917001814331423,
        0.8717401485096066,
        1.0,
    ]
)
LIFT_FACTOR = 28.0
TIME_STEP = 0.01
COUPLING = 4.0
MOMENT_WEIGHT = 0.0625


def derivative_matrix():
    points = GLL_POINTS
    barycentric = np.ones(8)
    for j in range(8):
        for m in range(8):
            if m != j:
                barycentric[j] = barycentric[j] / (points[j] - points[m])
    matrix = np.zeros((8, 8))
    for i in range(8):
        for j in range(8):
            if i != j:
                matrix[i, j] = barycentric[j] / barycentric[i] / (points[i] - points[j])
        matrix[i, i] = -np.sum(matrix[i])
    return matrix


def kron_tables():
    matrix = derivative_matrix().T
    node = np.arange(NODES)
    spreads = [matrix[:, node // 64], matrix[:, node // 8 % 8], matrix[:, node % 8]]
    spreads = lax.optimization_barrier([jnp.asarray(t, jnp.float32) for t in spreads])
    row = lax.broadcasted_iota(jnp.int32, (NODES, NODES), 0)
    col = lax.broadcasted_iota(jnp.int32, (NODES, NODES), 1)
    same_a = row // 64 == col // 64
    same_b = row // 8 % 8 == col // 8 % 8
    same_c = row % 8 == col % 8
    shape = (8, 8, 8, NODES)
    along_x = jnp.broadcast_to(spreads[0][:, None, None, :], shape).reshape(NODES, NODES)
    along_y = jnp.broadcast_to(spreads[1][None, :, None, :], shape).reshape(NODES, NODES)
    along_z = jnp.broadcast_to(spreads[2][None, None, :, :], shape).reshape(NODES, NODES)
    zero = jnp.zeros((), jnp.float32)
    return [
        jnp.where(same_b & same_c, along_x, zero),
        jnp.where(same_a & same_c, along_y, zero),
        jnp.where(same_a & same_b, along_z, zero),
    ]


def basis_table():
    points = GLL_POINTS
    centres = -1.0 + (2.0 * np.arange(SUB) + 1.0) / SUB
    values = np.ones((SUB, 8))
    for j in range(8):
        for m in range(8):
            if m != j:
                values[:, j] = values[:, j] * (centres - points[m]) / (points[j] - points[m])
    return np.asarray(values, dtype=np.float32)


def neighbours(lower, upper, axis):
    count = lax.axis_size(axis)
    if count == 1:
        return jnp.zeros_like(upper), jnp.zeros_like(lower)
    if count == 2:
        index = lax.axis_index(axis)
        sent = jnp.where(index == 0, upper, lower)
        got = lax.ppermute(sent, axis, [(0, 1), (1, 0)])
        zero = jnp.zeros_like(got)
        return jnp.where(index == 1, got, zero), jnp.where(index == 0, got, zero)
    from_below = lax.ppermute(upper, axis, [(i, i + 1) for i in range(count - 1)])
    from_above = lax.ppermute(lower, axis, [(i + 1, i) for i in range(count - 1)])
    return from_below, from_above


def source_cells(velocity, viscosity):
    below_x, above_x = neighbours(velocity[:, :1], velocity[:, -1:], "gx")
    below_y, above_y = neighbours(velocity[:, :, :1], velocity[:, :, -1:], "gy")
    below_z, above_z = neighbours(velocity[..., :1], velocity[..., -1:], "gz")
    centre = velocity.astype(jnp.float32)
    f32 = lambda t: t.astype(jnp.float32)
    plus_x = jnp.concatenate([centre[:, 1:], f32(above_x)], axis=1)
    minus_x = jnp.concatenate([f32(below_x), centre[:, :-1]], axis=1)
    plus_y = jnp.concatenate([centre[:, :, 1:], f32(above_y)], axis=2)
    minus_y = jnp.concatenate([f32(below_y), centre[:, :, :-1]], axis=2)
    plus_z = jnp.concatenate([centre[..., 1:], f32(above_z)], axis=3)
    minus_z = jnp.concatenate([f32(below_z), centre[..., :-1]], axis=3)
    grad_x = 0.5 * (plus_x - minus_x)
    grad_y = 0.5 * (plus_y - minus_y)
    grad_z = 0.5 * (plus_z - minus_z)
    laplace = plus_x + minus_x + plus_y + minus_y + plus_z + minus_z - 6.0 * centre
    curl_x = grad_y[2] - grad_z[1]
    curl_y = grad_z[0] - grad_x[2]
    curl_z = grad_x[1] - grad_y[0]
    lamb_x = curl_y * centre[2] - curl_z * centre[1]
    lamb_y = curl_z * centre[0] - curl_x * centre[2]
    lamb_z = curl_x * centre[1] - curl_y * centre[0]
    lamb = jnp.stack([lamb_x, lamb_y, lamb_z])
    return (viscosity[None] * laplace - lamb).astype(jnp.bfloat16)


def face_correction(inside, outside, normal, component):
    difference = inside - outside
    result = -0.5 * difference
    first = result[0] + 0.5 * normal * difference[component]
    chosen = result[component] + 0.5 * normal * difference[0]
    parts = [result[i] for i in range(4)]
    parts[0] = first
    parts[component] = chosen
    return LIFT_FACTOR * jnp.stack(parts)


def tendency(fields, tables):
    highest = lax.Precision.HIGHEST
    count = fields.shape[1]
    grads = [jnp.dot(fields[0], table, precision=highest) for table in tables]
    divergence = (
        jnp.dot(fields[1], tables[0], precision=highest)
        + jnp.dot(fields[2], tables[1], precision=highest)
        + jnp.dot(fields[3], tables[2], precision=highest)
    )
    result = jnp.stack([-divergence, -grads[0], -grads[1], -grads[2]])

    face = 64
    below_x, above_x = neighbours(fields[..., :face], fields[..., NODES - face :], "gx")
    below_y, above_y = neighbours(fields, fields, "gy")
    below_z, above_z = neighbours(fields[:, :1], fields[:, count - 1 :], "gz")
    outer_lower_x = jnp.pad(below_x, ((0, 0), (0, 0), (0, NODES - face)))
    outer_upper_x = jnp.pad(above_x, ((0, 0), (0, 0), (NODES - face, 0)))
    outer_lower_y = jnp.roll(below_y, -56, axis=2)
    outer_upper_y = jnp.roll(above_y, 56, axis=2)
    outer_lower_z = jnp.roll(jnp.concatenate([below_z, fields[:, :-1]], axis=1), -7, axis=2)
    outer_upper_z = jnp.roll(jnp.concatenate([fields[:, 1:], above_z], axis=1), 7, axis=2)

    node = jnp.arange(NODES, dtype=jnp.int32)
    places = (node // 64, node // 8 % 8, node % 8)
    faces = (
        (outer_lower_x, outer_upper_x),
        (outer_lower_y, outer_upper_y),
        (outer_lower_z, outer_upper_z),
    )
    for direction, (low_out, high_out) in enumerate(faces):
        place = places[direction]
        low_corr = face_correction(fields, low_out, -1.0, direction + 1)
        high_corr = face_correction(fields, high_out, 1.0, direction + 1)
        added = jnp.where(place == 0, low_corr, jnp.where(place == 7, high_corr, 0.0))
        result = result + added
    return result


def runge_kutta(fields, forcing):
    tables = kron_tables()
    coupled = jnp.concatenate([jnp.zeros_like(forcing[:1]), COUPLING * forcing])
    step = lambda f: tendency(f, tables) + coupled
    first = tendency(fields, tables)
    section_one = fields + TIME_STEP * (first + coupled)
    section_two = 0.75 * fields + 0.25 * (section_one + TIME_STEP * step(section_one))
    return 1.0 / 3.0 * fields + 2.0 / 3.0 * (section_two + TIME_STEP * step(section_two))


def pick_columns(index, table):
    levels = jnp.arange(table.shape[1], dtype=jnp.int32)
    chosen = jnp.where(index[None, None, :] == levels[None, :, None], table[:, :, None], 0.0)
    return jnp.sum(chosen, axis=1)


def on_device_body(velocity, eddy_viscosity, cell_owner, cell_element, cell_position, acoustic_state):
    sources = source_cells(velocity, eddy_viscosity)
    cell_count = sources.shape[1] * sources.shape[2] * sources.shape[3]
    flat_source = sources.reshape(3, cell_count).astype(jnp.float32)
    owners = cell_owner.reshape(cell_count)
    elements = cell_element.reshape(cell_count)
    positions = cell_position.reshape(cell_count)
    owner_count = lax.axis_size("gx")
    capacity = 3 * cell_count // (2 * owner_count)
    owner_hot = (owners[:, None] == jnp.arange(owner_count, dtype=jnp.int32)[None, :]).astype(
        jnp.int32
    )
    earlier = jnp.cumsum(owner_hot, axis=0) - owner_hot
    order_within = jnp.sum(earlier * owner_hot, axis=1)
    slot_index = owners * capacity + order_within
    subcells = SUB * SUB * SUB
    ident = (elements * subcells + positions).astype(jnp.float32)
    payload = jnp.concatenate([flat_source, ident[None]], axis=0)
    send = (
        jnp.zeros((4, owner_count * capacity), jnp.float32)
        .at[:, slot_index]
        .set(payload)
        .reshape(4, owner_count, capacity)
    )
    send = jnp.transpose(send, (1, 0, 2)).reshape(owner_count, 4 * capacity)
    got = lax.all_to_all(send, "gx", split_axis=0, concat_axis=0, tiled=True)
    got = jnp.transpose(got.reshape(owner_count, 4, capacity), (1, 0, 2)).reshape(
        4, owner_count * capacity
    )
    got_source = got[:3].astype(jnp.bfloat16)
    got_ident = got[3].astype(jnp.int32)
    got_element = got_ident // subcells
    got_position = got_ident % subcells

    values = jnp.asarray(basis_table().T)
    along_a = pick_columns(got_position // (SUB * SUB), values)
    along_b = pick_columns(got_position // SUB % SUB, values)
    along_c = pick_columns(got_position % SUB, values)
    rows = got_position.shape[0]
    node_columns = (
        along_a[:, None, None, :] * along_b[None, :, None, :] * along_c[None, None, :, :]
    ).reshape(NODES, rows).astype(jnp.bfloat16)

    local_elems = acoustic_state.shape[1] * acoustic_state.shape[2] * acoustic_state.shape[3]
    element_hot = got_element[None, :] == jnp.arange(local_elems, dtype=jnp.int32)[:, None]
    weighted = jnp.where(element_hot[None], got_source[:, None, :], jnp.zeros((), jnp.bfloat16))
    weighted = weighted.reshape(3 * local_elems, rows)
    totals = lax.dot_general(
        weighted, node_columns, (((1,), (1,)), ((), ())), preferred_element_type=jnp.float32
    )
    forcing = (totals * MOMENT_WEIGHT).reshape(3, local_elems, NODES)
    moments = jnp.moveaxis(forcing, 0, 1).reshape(
        acoustic_state.shape[1:4] + (3, NODES)
    )

    fields = acoustic_state.reshape(4, local_elems, NODES)
    next_state = runge_kutta(fields, forcing).reshape(acoustic_state.shape)
    return (moments, next_state)


def solution(mesh):
    in_specs = (
        P(None, "gx", "gy", "gz"),
        P("gx", "gy", "gz"),
        P("gy", "gz", "gx", None),
        P("gy", "gz", "gx"),
        P("gy", "gz", "gx"),
        P(None, "gx", "gy", "gz", None),
    )
    out_specs = (P("gx", "gy", "gz", None, None), P(None, "gx", "gy", "gz", None))
    return jax.shard_map(
        on_device_body, mesh=mesh, in_specs=in_specs, out_specs=out_specs, check_vma=False
    )
```

```python
import jax
import jax.numpy as jnp
import numpy as np
from jax import lax
from jax.sharding import PartitionSpec as P


SUB = 16
NODES = 512


GLL_POINTS = np.array(
    [
        -1.0,
        -0.8717401485096066,
        -0.5917001814331423,
        -0.2092992179024789,
        0.2092992179024789,
        0.5917001814331423,
        0.8717401485096066,
        1.0,
    ]
)
LIFT_FACTOR = 28.0
TIME_STEP = 0.01
COUPLING = 4.0
MOMENT_WEIGHT = 0.0625


def derivative_matrix():
    points = GLL_POINTS
    barycentric = np.ones(8)
    for j in range(8):
        for m in range(8):
            if m != j:
                barycentric[j] = barycentric[j] / (points[j] - points[m])
    matrix = np.zeros((8, 8))
    for i in range(8):
        for j in range(8):
            if i != j:
                matrix[i, j] = barycentric[j] / barycentric[i] / (points[i] - points[j])
        matrix[i, i] = -np.sum(matrix[i])
    return matrix


def kron_tables():
    matrix = derivative_matrix().T
    node = np.arange(NODES)
    spreads = [matrix[:, node // 64], matrix[:, node // 8 % 8], matrix[:, node % 8]]
    spreads = lax.optimization_barrier([jnp.asarray(t, jnp.float32) for t in spreads])
    row = lax.broadcasted_iota(jnp.int32, (NODES, NODES), 0)
    col = lax.broadcasted_iota(jnp.int32, (NODES, NODES), 1)
    same_a = row // 64 == col // 64
    same_b = row // 8 % 8 == col // 8 % 8
    same_c = row % 8 == col % 8
    shape = (8, 8, 8, NODES)
    along_x = jnp.broadcast_to(spreads[0][:, None, None, :], shape).reshape(NODES, NODES)
    along_y = jnp.broadcast_to(spreads[1][None, :, None, :], shape).reshape(NODES, NODES)
    along_z = jnp.broadcast_to(spreads[2][None, None, :, :], shape).reshape(NODES, NODES)
    zero = jnp.zeros((), jnp.float32)
    return [
        jnp.where(same_b & same_c, along_x, zero),
        jnp.where(same_a & same_c, along_y, zero),
        jnp.where(same_a & same_b, along_z, zero),
    ]


def basis_table():
    points = GLL_POINTS
    centres = -1.0 + (2.0 * np.arange(SUB) + 1.0) / SUB
    values = np.ones((SUB, 8))
    for j in range(8):
        for m in range(8):
            if m != j:
                values[:, j] = values[:, j] * (centres - points[m]) / (points[j] - points[m])
    return np.asarray(values, dtype=np.float32)


def neighbours(lower, upper, axis):
    count = lax.axis_size(axis)
    if count == 1:
        return jnp.zeros_like(upper), jnp.zeros_like(lower)
    if count == 2:
        index = lax.axis_index(axis)
        sent = jnp.where(index == 0, upper, lower)
        got = lax.ppermute(sent, axis, [(0, 1), (1, 0)])
        zero = jnp.zeros_like(got)
        return jnp.where(index == 1, got, zero), jnp.where(index == 0, got, zero)
    from_below = lax.ppermute(upper, axis, [(i, i + 1) for i in range(count - 1)])
    from_above = lax.ppermute(lower, axis, [(i + 1, i) for i in range(count - 1)])
    return from_below, from_above


def source_cells(velocity, viscosity):
    below_x, above_x = neighbours(velocity[:, :1], velocity[:, -1:], "gx")
    below_y, above_y = neighbours(velocity[:, :, :1], velocity[:, :, -1:], "gy")
    below_z, above_z = neighbours(velocity[..., :1], velocity[..., -1:], "gz")
    centre = velocity.astype(jnp.float32)
    f32 = lambda t: t.astype(jnp.float32)
    plus_x = jnp.concatenate([centre[:, 1:], f32(above_x)], axis=1)
    minus_x = jnp.concatenate([f32(below_x), centre[:, :-1]], axis=1)
    plus_y = jnp.concatenate([centre[:, :, 1:], f32(above_y)], axis=2)
    minus_y = jnp.concatenate([f32(below_y), centre[:, :, :-1]], axis=2)
    plus_z = jnp.concatenate([centre[..., 1:], f32(above_z)], axis=3)
    minus_z = jnp.concatenate([f32(below_z), centre[..., :-1]], axis=3)
    grad_x = 0.5 * (plus_x - minus_x)
    grad_y = 0.5 * (plus_y - minus_y)
    grad_z = 0.5 * (plus_z - minus_z)
    laplace = plus_x + minus_x + plus_y + minus_y + plus_z + minus_z - 6.0 * centre
    curl_x = grad_y[2] - grad_z[1]
    curl_y = grad_z[0] - grad_x[2]
    curl_z = grad_x[1] - grad_y[0]
    lamb_x = curl_y * centre[2] - curl_z * centre[1]
    lamb_y = curl_z * centre[0] - curl_x * centre[2]
    lamb_z = curl_x * centre[1] - curl_y * centre[0]
    lamb = jnp.stack([lamb_x, lamb_y, lamb_z])
    return (viscosity[None] * laplace - lamb).astype(jnp.bfloat16)


def face_correction(inside, outside, normal, component):
    difference = inside - outside
    result = -0.5 * difference
    first = result[0] + 0.5 * normal * difference[component]
    chosen = result[component] + 0.5 * normal * difference[0]
    parts = [result[i] for i in range(4)]
    parts[0] = first
    parts[component] = chosen
    return LIFT_FACTOR * jnp.stack(parts)


def tendency(fields, tables):
    precision = lax.Precision.HIGH
    count = fields.shape[1]
    grad_table, div_table = tables
    grads = jnp.dot(fields[0], grad_table, precision=precision)
    grads = [grads[:, k * NODES : (k + 1) * NODES] for k in range(3)]
    velocity_rows = jnp.concatenate([fields[1], fields[2], fields[3]], axis=1)
    divergence = jnp.dot(velocity_rows, div_table, precision=precision)
    result = jnp.stack([-divergence, -grads[0], -grads[1], -grads[2]])

    face = 64
    below_x, above_x = neighbours(fields[..., :face], fields[..., NODES - face :], "gx")
    below_y, above_y = neighbours(fields, fields, "gy")
    below_z, above_z = neighbours(fields[:, :1], fields[:, count - 1 :], "gz")
    outer_lower_x = jnp.pad(below_x, ((0, 0), (0, 0), (0, NODES - face)))
    outer_upper_x = jnp.pad(above_x, ((0, 0), (0, 0), (NODES - face, 0)))
    outer_lower_y = jnp.roll(below_y, -56, axis=2)
    outer_upper_y = jnp.roll(above_y, 56, axis=2)
    outer_lower_z = jnp.roll(jnp.concatenate([below_z, fields[:, :-1]], axis=1), -7, axis=2)
    outer_upper_z = jnp.roll(jnp.concatenate([fields[:, 1:], above_z], axis=1), 7, axis=2)

    node = jnp.arange(NODES, dtype=jnp.int32)
    places = (node // 64, node // 8 % 8, node % 8)
    faces = (
        (outer_lower_x, outer_upper_x),
        (outer_lower_y, outer_upper_y),
        (outer_lower_z, outer_upper_z),
    )
    for direction, (low_out, high_out) in enumerate(faces):
        place = places[direction]
        low_corr = face_correction(fields, low_out, -1.0, direction + 1)
        high_corr = face_correction(fields, high_out, 1.0, direction + 1)
        added = jnp.where(place == 0, low_corr, jnp.where(place == 7, high_corr, 0.0))
        result = result + added
    return result


def runge_kutta(fields, forcing):
    parts = kron_tables()
    tables = (jnp.concatenate(parts, axis=1), jnp.concatenate(parts, axis=0))
    coupled = jnp.concatenate([jnp.zeros_like(forcing[:1]), COUPLING * forcing])
    step = lambda f: tendency(f, tables) + coupled
    first = tendency(fields, tables)
    section_one = fields + TIME_STEP * (first + coupled)
    section_two = 0.75 * fields + 0.25 * (section_one + TIME_STEP * step(section_one))
    return 1.0 / 3.0 * fields + 2.0 / 3.0 * (section_two + TIME_STEP * step(section_two))


def pick_columns(index, table):
    levels = jnp.arange(table.shape[1], dtype=jnp.int32)
    chosen = jnp.where(index[None, None, :] == levels[None, :, None], table[:, :, None], 0.0)
    return jnp.sum(chosen, axis=1)


def on_device_body(velocity, eddy_viscosity, cell_owner, cell_element, cell_position, acoustic_state):
    sources = source_cells(velocity, eddy_viscosity)
    cell_count = sources.shape[1] * sources.shape[2] * sources.shape[3]
    flat_source = sources.reshape(3, cell_count).astype(jnp.float32)
    owners = cell_owner.reshape(cell_count)
    elements = cell_element.reshape(cell_count)
    positions = cell_position.reshape(cell_count)
    owner_count = lax.axis_size("gx")
    capacity = 3 * cell_count // (2 * owner_count)
    subcells = SUB * SUB * SUB
    owner_hot = (owners[:, None] == jnp.arange(owner_count, dtype=jnp.int32)[None, :]).astype(
        jnp.int32
    )
    earlier = jnp.cumsum(owner_hot, axis=0) - owner_hot
    order_within = jnp.sum(earlier * owner_hot, axis=1)
    slot_index = owners * capacity + order_within
    ident = (elements * subcells + positions).astype(jnp.float32)
    payload = jnp.concatenate([flat_source, ident[None]], axis=0)
    send = (
        jnp.zeros((4, owner_count * capacity), jnp.float32)
        .at[:, slot_index]
        .set(payload)
        .reshape(4, owner_count, capacity)
    )
    send = jnp.transpose(send, (1, 0, 2)).reshape(owner_count, 4 * capacity)
    got = lax.all_to_all(send, "gx", split_axis=0, concat_axis=0, tiled=True)
    got = jnp.transpose(got.reshape(owner_count, 4, capacity), (1, 0, 2)).reshape(
        4, owner_count * capacity
    )
    got_source = got[:3].astype(jnp.bfloat16)
    got_ident = got[3].astype(jnp.int32)
    got_element = got_ident // subcells
    got_position = got_ident % subcells

    values = jnp.asarray(basis_table().T)
    along_a = pick_columns(got_position // (SUB * SUB), values)
    along_b = pick_columns(got_position // SUB % SUB, values)
    along_c = pick_columns(got_position % SUB, values)
    rows = got_position.shape[0]
    node_columns = (
        along_a[:, None, None, :] * along_b[None, :, None, :] * along_c[None, None, :, :]
    ).reshape(NODES, rows).astype(jnp.bfloat16)

    local_elems = acoustic_state.shape[1] * acoustic_state.shape[2] * acoustic_state.shape[3]
    element_hot = got_element[None, :] == jnp.arange(local_elems, dtype=jnp.int32)[:, None]
    weighted = jnp.where(element_hot[None], got_source[:, None, :], jnp.zeros((), jnp.bfloat16))
    weighted = weighted.reshape(3 * local_elems, rows)
    totals = lax.dot_general(
        weighted, node_columns, (((1,), (1,)), ((), ())), preferred_element_type=jnp.float32
    )
    forcing = (totals * MOMENT_WEIGHT).reshape(3, local_elems, NODES)
    moments = jnp.moveaxis(forcing, 0, 1).reshape(
        acoustic_state.shape[1:4] + (3, NODES)
    )

    fields = acoustic_state.reshape(4, local_elems, NODES)
    next_state = runge_kutta(fields, forcing).reshape(acoustic_state.shape)
    return (moments, next_state)


def solution(mesh):
    in_specs = (
        P(None, "gx", "gy", "gz"),
        P("gx", "gy", "gz"),
        P("gy", "gz", "gx", None),
        P("gy", "gz", "gx"),
        P("gy", "gz", "gx"),
        P(None, "gx", "gy", "gz", None),
    )
    out_specs = (P("gx", "gy", "gz", None, None), P(None, "gx", "gy", "gz", None))
    return jax.shard_map(
        on_device_body, mesh=mesh, in_specs=in_specs, out_specs=out_specs, check_vma=False
    )
```

```python
import jax
import jax.numpy as jnp
import numpy as np
from jax import lax
from jax.sharding import PartitionSpec as P


SUB = 16
NODES = 512


GLL_POINTS = np.array(
    [
        -1.0,
        -0.8717401485096066,
        -0.5917001814331423,
        -0.2092992179024789,
        0.2092992179024789,
        0.5917001814331423,
        0.8717401485096066,
        1.0,
    ]
)
LIFT_FACTOR = 28.0
TIME_STEP = 0.01
COUPLING = 4.0
MOMENT_WEIGHT = 0.0625


def derivative_matrix():
    points = GLL_POINTS
    barycentric = np.ones(8)
    for j in range(8):
        for m in range(8):
            if m != j:
                barycentric[j] = barycentric[j] / (points[j] - points[m])
    matrix = np.zeros((8, 8))
    for i in range(8):
        for j in range(8):
            if i != j:
                matrix[i, j] = barycentric[j] / barycentric[i] / (points[i] - points[j])
        matrix[i, i] = -np.sum(matrix[i])
    return matrix


def kron_tables():
    matrix = derivative_matrix().T
    node = np.arange(NODES)
    spreads = [matrix[:, node // 64], matrix[:, node // 8 % 8], matrix[:, node % 8]]
    spreads = lax.optimization_barrier([jnp.asarray(t, jnp.float32) for t in spreads])
    row = lax.broadcasted_iota(jnp.int32, (NODES, NODES), 0)
    col = lax.broadcasted_iota(jnp.int32, (NODES, NODES), 1)
    same_a = row // 64 == col // 64
    same_b = row // 8 % 8 == col // 8 % 8
    same_c = row % 8 == col % 8
    shape = (8, 8, 8, NODES)
    along_x = jnp.broadcast_to(spreads[0][:, None, None, :], shape).reshape(NODES, NODES)
    along_y = jnp.broadcast_to(spreads[1][None, :, None, :], shape).reshape(NODES, NODES)
    along_z = jnp.broadcast_to(spreads[2][None, None, :, :], shape).reshape(NODES, NODES)
    zero = jnp.zeros((), jnp.float32)
    return [
        jnp.where(same_b & same_c, along_x, zero),
        jnp.where(same_a & same_c, along_y, zero),
        jnp.where(same_a & same_b, along_z, zero),
    ]


def basis_table():
    points = GLL_POINTS
    centres = -1.0 + (2.0 * np.arange(SUB) + 1.0) / SUB
    values = np.ones((SUB, 8))
    for j in range(8):
        for m in range(8):
            if m != j:
                values[:, j] = values[:, j] * (centres - points[m]) / (points[j] - points[m])
    return np.asarray(values, dtype=np.float32)


def neighbours(lower, upper, axis):
    count = lax.axis_size(axis)
    if count == 1:
        return jnp.zeros_like(upper), jnp.zeros_like(lower)
    if count == 2:
        index = lax.axis_index(axis)
        sent = jnp.where(index == 0, upper, lower)
        got = lax.ppermute(sent, axis, [(0, 1), (1, 0)])
        zero = jnp.zeros_like(got)
        return jnp.where(index == 1, got, zero), jnp.where(index == 0, got, zero)
    from_below = lax.ppermute(upper, axis, [(i, i + 1) for i in range(count - 1)])
    from_above = lax.ppermute(lower, axis, [(i + 1, i) for i in range(count - 1)])
    return from_below, from_above


def source_cells(velocity, viscosity):
    below_x, above_x = neighbours(velocity[:, :1], velocity[:, -1:], "gx")
    below_y, above_y = neighbours(velocity[:, :, :1], velocity[:, :, -1:], "gy")
    below_z, above_z = neighbours(velocity[..., :1], velocity[..., -1:], "gz")
    centre = velocity.astype(jnp.float32)
    f32 = lambda t: t.astype(jnp.float32)
    plus_x = jnp.concatenate([centre[:, 1:], f32(above_x)], axis=1)
    minus_x = jnp.concatenate([f32(below_x), centre[:, :-1]], axis=1)
    plus_y = jnp.concatenate([centre[:, :, 1:], f32(above_y)], axis=2)
    minus_y = jnp.concatenate([f32(below_y), centre[:, :, :-1]], axis=2)
    plus_z = jnp.concatenate([centre[..., 1:], f32(above_z)], axis=3)
    minus_z = jnp.concatenate([f32(below_z), centre[..., :-1]], axis=3)
    grad_x = 0.5 * (plus_x - minus_x)
    grad_y = 0.5 * (plus_y - minus_y)
    grad_z = 0.5 * (plus_z - minus_z)
    laplace = plus_x + minus_x + plus_y + minus_y + plus_z + minus_z - 6.0 * centre
    curl_x = grad_y[2] - grad_z[1]
    curl_y = grad_z[0] - grad_x[2]
    curl_z = grad_x[1] - grad_y[0]
    lamb_x = curl_y * centre[2] - curl_z * centre[1]
    lamb_y = curl_z * centre[0] - curl_x * centre[2]
    lamb_z = curl_x * centre[1] - curl_y * centre[0]
    lamb = jnp.stack([lamb_x, lamb_y, lamb_z])
    return (viscosity[None] * laplace - lamb).astype(jnp.bfloat16)


def face_correction(inside, outside, normal, component):
    difference = inside - outside
    result = -0.5 * difference
    first = result[0] + 0.5 * normal * difference[component]
    chosen = result[component] + 0.5 * normal * difference[0]
    parts = [result[i] for i in range(4)]
    parts[0] = first
    parts[component] = chosen
    return LIFT_FACTOR * jnp.stack(parts)


def tendency(fields, tables):
    precision = lax.Precision.HIGH
    count = fields.shape[1]
    grad_table, div_table = tables
    grads = jnp.dot(fields[0], grad_table, precision=precision)
    grads = [grads[:, k * NODES : (k + 1) * NODES] for k in range(3)]
    velocity_rows = jnp.concatenate([fields[1], fields[2], fields[3]], axis=1)
    divergence = jnp.dot(velocity_rows, div_table, precision=precision)
    result = jnp.stack([-divergence, -grads[0], -grads[1], -grads[2]])

    face = 64
    below_x, above_x = neighbours(fields[..., :face], fields[..., NODES - face :], "gx")
    below_y, above_y = neighbours(fields, fields, "gy")
    below_z, above_z = neighbours(fields[:, :1], fields[:, count - 1 :], "gz")
    outer_lower_x = jnp.pad(below_x, ((0, 0), (0, 0), (0, NODES - face)))
    outer_upper_x = jnp.pad(above_x, ((0, 0), (0, 0), (NODES - face, 0)))
    outer_lower_y = jnp.roll(below_y, -56, axis=2)
    outer_upper_y = jnp.roll(above_y, 56, axis=2)
    outer_lower_z = jnp.roll(jnp.concatenate([below_z, fields[:, :-1]], axis=1), -7, axis=2)
    outer_upper_z = jnp.roll(jnp.concatenate([fields[:, 1:], above_z], axis=1), 7, axis=2)

    node = jnp.arange(NODES, dtype=jnp.int32)
    places = (node // 64, node // 8 % 8, node % 8)
    faces = (
        (outer_lower_x, outer_upper_x),
        (outer_lower_y, outer_upper_y),
        (outer_lower_z, outer_upper_z),
    )
    for direction, (low_out, high_out) in enumerate(faces):
        place = places[direction]
        low_corr = face_correction(fields, low_out, -1.0, direction + 1)
        high_corr = face_correction(fields, high_out, 1.0, direction + 1)
        added = jnp.where(place == 0, low_corr, jnp.where(place == 7, high_corr, 0.0))
        result = result + added
    return result


def runge_kutta(fields, forcing):
    parts = kron_tables()
    tables = (jnp.concatenate(parts, axis=1), jnp.concatenate(parts, axis=0))
    coupled = jnp.concatenate([jnp.zeros_like(forcing[:1]), COUPLING * forcing])
    step = lambda f: tendency(f, tables) + coupled
    first = tendency(fields, tables)
    section_one = fields + TIME_STEP * (first + coupled)
    section_two = 0.75 * fields + 0.25 * (section_one + TIME_STEP * step(section_one))
    return 1.0 / 3.0 * fields + 2.0 / 3.0 * (section_two + TIME_STEP * step(section_two))


def on_device_body(velocity, eddy_viscosity, cell_owner, cell_element, cell_position, acoustic_state):
    sources = source_cells(velocity, eddy_viscosity)
    cell_count = sources.shape[1] * sources.shape[2] * sources.shape[3]
    flat_source = sources.reshape(3, cell_count).astype(jnp.float32)
    owners = cell_owner.reshape(cell_count)
    elements = cell_element.reshape(cell_count)
    positions = cell_position.reshape(cell_count)
    owner_count = lax.axis_size("gx")
    capacity = 3 * cell_count // (2 * owner_count)
    subcells = SUB * SUB * SUB
    owner_hot = (owners[:, None] == jnp.arange(owner_count, dtype=jnp.int32)[None, :]).astype(
        jnp.int32
    )
    earlier = jnp.cumsum(owner_hot, axis=0) - owner_hot
    order_within = jnp.sum(earlier * owner_hot, axis=1)
    slot_index = owners * capacity + order_within
    ident = (elements * subcells + positions).astype(jnp.float32)
    payload = jnp.concatenate([flat_source, ident[None]], axis=0)
    send = (
        jnp.zeros((4, owner_count * capacity), jnp.float32)
        .at[:, slot_index]
        .set(payload)
        .reshape(4, owner_count, capacity)
    )
    send = jnp.transpose(send, (1, 0, 2)).reshape(owner_count, 4 * capacity)
    got = lax.all_to_all(send, "gx", split_axis=0, concat_axis=0, tiled=True)
    got = jnp.transpose(got.reshape(owner_count, 4, capacity), (1, 0, 2)).reshape(
        4, owner_count * capacity
    )
    got_source = got[:3].astype(jnp.bfloat16)
    got_ident = got[3].astype(jnp.int32)
    got_element = got_ident // subcells
    got_position = got_ident % subcells

    values = jnp.asarray(basis_table().T)
    index = jnp.stack([got_position // (SUB * SUB), got_position // SUB % SUB, got_position % SUB])
    levels = jnp.arange(SUB, dtype=jnp.int32)
    chosen = jnp.where(
        index[:, None, None, :] == levels[None, None, :, None], values[None, :, :, None], 0.0
    )
    along_a, along_b, along_c = jnp.sum(chosen, axis=2)
    rows = got_position.shape[0]
    node_columns = (
        along_a[:, None, None, :] * along_b[None, :, None, :] * along_c[None, None, :, :]
    ).reshape(NODES, rows).astype(jnp.bfloat16)

    local_elems = acoustic_state.shape[1] * acoustic_state.shape[2] * acoustic_state.shape[3]
    element_hot = got_element[None, :] == jnp.arange(local_elems, dtype=jnp.int32)[:, None]
    weighted = jnp.where(element_hot[None], got_source[:, None, :], jnp.zeros((), jnp.bfloat16))
    weighted = weighted.reshape(3 * local_elems, rows)
    totals = lax.dot_general(
        weighted, node_columns, (((1,), (1,)), ((), ())), preferred_element_type=jnp.float32
    )
    forcing = (totals * MOMENT_WEIGHT).reshape(3, local_elems, NODES)
    moments = jnp.moveaxis(forcing, 0, 1).reshape(
        acoustic_state.shape[1:4] + (3, NODES)
    )

    fields = acoustic_state.reshape(4, local_elems, NODES)
    next_state = runge_kutta(fields, forcing).reshape(acoustic_state.shape)
    return (moments, next_state)


def solution(mesh):
    in_specs = (
        P(None, "gx", "gy", "gz"),
        P("gx", "gy", "gz"),
        P("gy", "gz", "gx", None),
        P("gy", "gz", "gx"),
        P("gy", "gz", "gx"),
        P(None, "gx", "gy", "gz", None),
    )
    out_specs = (P("gx", "gy", "gz", None, None), P(None, "gx", "gy", "gz", None))
    return jax.shard_map(
        on_device_body, mesh=mesh, in_specs=in_specs, out_specs=out_specs, check_vma=False
    )
```

```python
import jax
import jax.numpy as jnp
import numpy as np
from jax import lax
from jax.sharding import PartitionSpec as P


SUB = 16
NODES = 512


GLL_POINTS = np.array(
    [
        -1.0,
        -0.8717401485096066,
        -0.5917001814331423,
        -0.2092992179024789,
        0.2092992179024789,
        0.5917001814331423,
        0.8717401485096066,
        1.0,
    ]
)
LIFT_FACTOR = 28.0
TIME_STEP = 0.01
COUPLING = 4.0
MOMENT_WEIGHT = 0.0625


def derivative_matrix():
    points = GLL_POINTS
    barycentric = np.ones(8)
    for j in range(8):
        for m in range(8):
            if m != j:
                barycentric[j] = barycentric[j] / (points[j] - points[m])
    matrix = np.zeros((8, 8))
    for i in range(8):
        for j in range(8):
            if i != j:
                matrix[i, j] = barycentric[j] / barycentric[i] / (points[i] - points[j])
        matrix[i, i] = -np.sum(matrix[i])
    return matrix


def kron_tables():
    matrix = derivative_matrix().T
    node = np.arange(NODES)
    spreads = [matrix[:, node // 64], matrix[:, node // 8 % 8], matrix[:, node % 8]]
    spreads = lax.optimization_barrier([jnp.asarray(t, jnp.float32) for t in spreads])
    row = lax.broadcasted_iota(jnp.int32, (NODES, NODES), 0)
    col = lax.broadcasted_iota(jnp.int32, (NODES, NODES), 1)
    same_a = row // 64 == col // 64
    same_b = row // 8 % 8 == col // 8 % 8
    same_c = row % 8 == col % 8
    shape = (8, 8, 8, NODES)
    along_x = jnp.broadcast_to(spreads[0][:, None, None, :], shape).reshape(NODES, NODES)
    along_y = jnp.broadcast_to(spreads[1][None, :, None, :], shape).reshape(NODES, NODES)
    along_z = jnp.broadcast_to(spreads[2][None, None, :, :], shape).reshape(NODES, NODES)
    zero = jnp.zeros((), jnp.float32)
    return [
        jnp.where(same_b & same_c, along_x, zero),
        jnp.where(same_a & same_c, along_y, zero),
        jnp.where(same_a & same_b, along_z, zero),
    ]


def basis_table():
    points = GLL_POINTS
    centres = -1.0 + (2.0 * np.arange(SUB) + 1.0) / SUB
    values = np.ones((SUB, 8))
    for j in range(8):
        for m in range(8):
            if m != j:
                values[:, j] = values[:, j] * (centres - points[m]) / (points[j] - points[m])
    return np.asarray(values, dtype=np.float32)


def neighbours(lower, upper, axis):
    count = lax.axis_size(axis)
    if count == 1:
        return jnp.zeros_like(upper), jnp.zeros_like(lower)
    if count == 2:
        index = lax.axis_index(axis)
        sent = jnp.where(index == 0, upper, lower)
        got = lax.ppermute(sent, axis, [(0, 1), (1, 0)])
        zero = jnp.zeros_like(got)
        return jnp.where(index == 1, got, zero), jnp.where(index == 0, got, zero)
    from_below = lax.ppermute(upper, axis, [(i, i + 1) for i in range(count - 1)])
    from_above = lax.ppermute(lower, axis, [(i + 1, i) for i in range(count - 1)])
    return from_below, from_above


def source_cells(velocity, viscosity):
    below_x, above_x = neighbours(velocity[:, :1], velocity[:, -1:], "gx")
    below_y, above_y = neighbours(velocity[:, :, :1], velocity[:, :, -1:], "gy")
    below_z, above_z = neighbours(velocity[..., :1], velocity[..., -1:], "gz")
    centre = velocity.astype(jnp.float32)
    f32 = lambda t: t.astype(jnp.float32)
    plus_x = jnp.concatenate([centre[:, 1:], f32(above_x)], axis=1)
    minus_x = jnp.concatenate([f32(below_x), centre[:, :-1]], axis=1)
    plus_y = jnp.concatenate([centre[:, :, 1:], f32(above_y)], axis=2)
    minus_y = jnp.concatenate([f32(below_y), centre[:, :, :-1]], axis=2)
    plus_z = jnp.concatenate([centre[..., 1:], f32(above_z)], axis=3)
    minus_z = jnp.concatenate([f32(below_z), centre[..., :-1]], axis=3)
    grad_x = 0.5 * (plus_x - minus_x)
    grad_y = 0.5 * (plus_y - minus_y)
    grad_z = 0.5 * (plus_z - minus_z)
    laplace = plus_x + minus_x + plus_y + minus_y + plus_z + minus_z - 6.0 * centre
    curl_x = grad_y[2] - grad_z[1]
    curl_y = grad_z[0] - grad_x[2]
    curl_z = grad_x[1] - grad_y[0]
    lamb_x = curl_y * centre[2] - curl_z * centre[1]
    lamb_y = curl_z * centre[0] - curl_x * centre[2]
    lamb_z = curl_x * centre[1] - curl_y * centre[0]
    lamb = jnp.stack([lamb_x, lamb_y, lamb_z])
    return (viscosity[None] * laplace - lamb).astype(jnp.bfloat16)


def face_correction(inside, outside, normal, component):
    difference = inside - outside
    result = -0.5 * difference
    first = result[0] + 0.5 * normal * difference[component]
    chosen = result[component] + 0.5 * normal * difference[0]
    parts = [result[i] for i in range(4)]
    parts[0] = first
    parts[component] = chosen
    return LIFT_FACTOR * jnp.stack(parts)


def tendency(fields, tables):
    precision = lax.Precision.HIGH
    count = fields.shape[1]
    grad_table, div_table = tables
    grads = jnp.dot(fields[0], grad_table, precision=precision)
    grads = [grads[:, k * NODES : (k + 1) * NODES] for k in range(3)]
    velocity_rows = jnp.concatenate([fields[1], fields[2], fields[3]], axis=1)
    divergence = jnp.dot(velocity_rows, div_table, precision=precision)
    result = jnp.stack([-divergence, -grads[0], -grads[1], -grads[2]])

    face = 64
    below_x, above_x = neighbours(fields[..., :face], fields[..., NODES - face :], "gx")
    below_y, above_y = neighbours(fields, fields, "gy")
    below_z, above_z = neighbours(fields[:, :1], fields[:, count - 1 :], "gz")
    outer_lower_x = jnp.pad(below_x, ((0, 0), (0, 0), (0, NODES - face)))
    outer_upper_x = jnp.pad(above_x, ((0, 0), (0, 0), (NODES - face, 0)))
    outer_lower_y = jnp.roll(below_y, -56, axis=2)
    outer_upper_y = jnp.roll(above_y, 56, axis=2)
    outer_lower_z = jnp.roll(jnp.concatenate([below_z, fields[:, :-1]], axis=1), -7, axis=2)
    outer_upper_z = jnp.roll(jnp.concatenate([fields[:, 1:], above_z], axis=1), 7, axis=2)

    node = jnp.arange(NODES, dtype=jnp.int32)
    places = (node // 64, node // 8 % 8, node % 8)
    faces = (
        (outer_lower_x, outer_upper_x),
        (outer_lower_y, outer_upper_y),
        (outer_lower_z, outer_upper_z),
    )
    for direction, (low_out, high_out) in enumerate(faces):
        place = places[direction]
        low_corr = face_correction(fields, low_out, -1.0, direction + 1)
        high_corr = face_correction(fields, high_out, 1.0, direction + 1)
        added = jnp.where(place == 0, low_corr, jnp.where(place == 7, high_corr, 0.0))
        result = result + added
    return result


def runge_kutta(fields, forcing):
    parts = kron_tables()
    tables = (jnp.concatenate(parts, axis=1), jnp.concatenate(parts, axis=0))
    coupled = jnp.concatenate([jnp.zeros_like(forcing[:1]), COUPLING * forcing])
    step = lambda f: tendency(f, tables) + coupled
    first = tendency(fields, tables)
    section_one = fields + TIME_STEP * (first + coupled)
    section_two = 0.75 * fields + 0.25 * (section_one + TIME_STEP * step(section_one))
    return 1.0 / 3.0 * fields + 2.0 / 3.0 * (section_two + TIME_STEP * step(section_two))


def pick_columns(index, table):
    levels = jnp.arange(table.shape[1], dtype=jnp.int32)
    chosen = jnp.where(index[None, None, :] == levels[None, :, None], table[:, :, None], 0.0)
    return jnp.sum(chosen, axis=1)


def on_device_body(velocity, eddy_viscosity, cell_owner, cell_element, cell_position, acoustic_state):
    sources = source_cells(velocity, eddy_viscosity)
    cell_count = sources.shape[1] * sources.shape[2] * sources.shape[3]
    flat_source = sources.reshape(3, cell_count).astype(jnp.float32)
    owners = cell_owner.reshape(cell_count)
    elements = cell_element.reshape(cell_count)
    positions = cell_position.reshape(cell_count)
    owner_count = lax.axis_size("gx")
    capacity = 3 * cell_count // (2 * owner_count)
    owner_hot = (owners[:, None] == jnp.arange(owner_count, dtype=jnp.int32)[None, :]).astype(
        jnp.int32
    )
    earlier = jnp.cumsum(owner_hot, axis=0) - owner_hot
    order_within = jnp.sum(earlier * owner_hot, axis=1)
    slot_index = owners * capacity + order_within
    ident_high = (elements * SUB + positions // (SUB * SUB)).astype(jnp.float32)
    ident_low = (positions % (SUB * SUB)).astype(jnp.float32)
    payload = jnp.concatenate([flat_source, ident_high[None], ident_low[None]], axis=0)
    payload = payload.astype(jnp.bfloat16)
    send = (
        jnp.zeros((5, owner_count * capacity), jnp.bfloat16)
        .at[:, slot_index]
        .set(payload)
        .reshape(5, owner_count, capacity)
    )
    send = jnp.transpose(send, (1, 0, 2)).reshape(owner_count, 5 * capacity)
    got = lax.all_to_all(send, "gx", split_axis=0, concat_axis=0, tiled=True)
    got = jnp.transpose(got.reshape(owner_count, 5, capacity), (1, 0, 2)).reshape(
        5, owner_count * capacity
    )
    got_source = got[:3]
    got_high = got[3].astype(jnp.int32)
    got_element = got_high // SUB
    got_position = got_high % SUB * (SUB * SUB) + got[4].astype(jnp.int32)

    values = jnp.asarray(basis_table().T)
    along_a = pick_columns(got_position // (SUB * SUB), values)
    along_b = pick_columns(got_position // SUB % SUB, values)
    along_c = pick_columns(got_position % SUB, values)
    rows = got_position.shape[0]
    node_columns = (
        along_a[:, None, None, :] * along_b[None, :, None, :] * along_c[None, None, :, :]
    ).reshape(NODES, rows).astype(jnp.bfloat16)

    local_elems = acoustic_state.shape[1] * acoustic_state.shape[2] * acoustic_state.shape[3]
    element_hot = got_element[None, :] == jnp.arange(local_elems, dtype=jnp.int32)[:, None]
    weighted = jnp.where(element_hot[None], got_source[:, None, :], jnp.zeros((), jnp.bfloat16))
    weighted = weighted.reshape(3 * local_elems, rows)
    totals = lax.dot_general(
        weighted, node_columns, (((1,), (1,)), ((), ())), preferred_element_type=jnp.float32
    )
    forcing = (totals * MOMENT_WEIGHT).reshape(3, local_elems, NODES)
    moments = jnp.moveaxis(forcing, 0, 1).reshape(
        acoustic_state.shape[1:4] + (3, NODES)
    )

    fields = acoustic_state.reshape(4, local_elems, NODES)
    next_state = runge_kutta(fields, forcing).reshape(acoustic_state.shape)
    return (moments, next_state)


def solution(mesh):
    in_specs = (
        P(None, "gx", "gy", "gz"),
        P("gx", "gy", "gz"),
        P("gy", "gz", "gx", None),
        P("gy", "gz", "gx"),
        P("gy", "gz", "gx"),
        P(None, "gx", "gy", "gz", None),
    )
    out_specs = (P("gx", "gy", "gz", None, None), P(None, "gx", "gy", "gz", None))
    return jax.shard_map(
        on_device_body, mesh=mesh, in_specs=in_specs, out_specs=out_specs, check_vma=False
    )
```
